256 devices in a mesh: row: 16 (over y, x), col: 16 (over z, core).
Axes of the slice: x: 4, y: 4, z: 8, core: 2. Of those that a mesh axis runs over, the one named last changes fastest.
Arguments:
- intensity: int32 [512, 4096], P('row', 'col'), may hold values from 0 to 255
- agreement: int32 [4, 512, 4096], P(None, 'row', 'col'), may hold values from 0 to 8
- basis_block: float32 [128, 512, 4096], P(None, 'row', 'col'), may hold values from -2000 to 2000
Outputs:
- ortho_block: float32 [128, 512, 4096], P(None, 'row', 'col')
- upper_factor: float32 [128, 128], replicated
The draws below stay inside these ranges and needn't reach their ends.
All inputs are finite; a program needn't handle non-finite values.
Results may differ from the reference program's by a relative error of at most 0.00014.
Values sent between devices are 32-bit elements; how exact they have to be, the bound alone decides.
No kernel may reach another device: no remote copies, remote signals or barrier semaphores. Data moves between devices by JAX's collectives and lax.ppermute only.
A program may use at most 64 MiB of HBM per device.

```python
import math
import jax
import jax.numpy as jnp
from jax import lax

K = 128
NR = 512
NC = 4096


def draw_basis_block(key, part):
    first, second, third = jax.random.split(key, 3)
    vector_scale = jnp.exp(jax.random.uniform(second, (K, 1, 1), jnp.float32, 0.0, math.log(10.0)))
    pixel_scale = jnp.exp(jax.random.uniform(third, (1, NR, NC), jnp.float32, 0.0, math.log(10.0)))
    row_pos = jnp.arange(NR, dtype=jnp.float32)[:, None] / NR
    col_pos = jnp.arange(NC, dtype=jnp.float32)[None, :] / NC
    trend = jnp.exp(0.5 * math.log(3.0) * (row_pos + col_pos))[None]
    base = jnp.clip(jax.random.normal(first, (K, NR, NC), jnp.float32), -6.0, 6.0)
    return (base * vector_scale * pixel_scale * trend).astype(jnp.float32)


def plant(values, rng, least, top_value):
    place = [jax.random.randint(jax.random.fold_in(rng, axis), (), 0, length) for axis, length in enumerate(values.shape)]
    main_axis = values.shape.index(max(values.shape))
    beside = place[:main_axis] + [(place[main_axis] + 1) % values.shape[main_axis]] + place[main_axis + 1:]
    return values.at[tuple(place)].set(least).at[tuple(beside)].set(top_value)


def setup_inputs(seed: int = 0) -> dict:
    seeds = jax.random.split(jax.random.key(seed), 4)
    return {
        "intensity": plant(jax.random.randint(seeds[0], (NR, NC), 0, 256), jax.random.fold_in(seeds[0], 1), 0, 255).astype(jnp.int32),
        "agreement": plant(jax.random.randint(seeds[1], (4, NR, NC), 0, 9), jax.random.fold_in(seeds[1], 1), 0, 8).astype(jnp.int32),
        "basis_block": draw_basis_block(jax.random.fold_in(seeds[3], 71), 0),
    }


INV_SIGMA = 1.0 / 40.0
NEIGHBOURS = ((0, 1, 0, 1, 1.0 / 9.0), (0, -1, 0, 0, 1.0 / 9.0), (1, 0, 1, 1, 1.0 / 9.0), (-1, 0, 1, 0, 1.0 / 9.0), (1, 1, 2, 1, 1.0 / 18.0), (-1, -1, 2, 0, 1.0 / 18.0), (1, -1, 3, 1, 1.0 / 18.0), (-1, 1, 3, 0, 1.0 / 18.0))

def shifted(array, step_row, step_col):
    height = array.shape[-2]
    width = array.shape[-1]
    return array[..., 1 + step_row:height - 1 + step_row, 1 + step_col:width - 1 + step_col]

def cropped(array, cycle):
    if cycle == 0:
        return array
    return array[..., cycle:-cycle, cycle:-cycle]

def neighbour_weights(levels, counts, inside):
    center = shifted(levels, 0, 0)
    center_in = shifted(inside, 0, 0)
    result = []
    for step_row, step_col, channel, at_center, factor in NEIGHBOURS:
        other = shifted(levels, step_row, step_col)
        if at_center == 1:
            source = shifted(counts[channel], 0, 0)
        else:
            source = shifted(counts[channel], step_row, step_col)
        gap = (center - other) * INV_SIGMA
        result.append((1.0 + source) * factor * jnp.exp(-gap * gap) * center_in * shifted(inside, step_row, step_col))
    return result

def degree_scales(weights):
    degree = weights[0]
    for weight in weights[1:]:
        degree = degree + weight
    return lax.rsqrt(1.0 + degree)

def apply_once(values_in, weights, scales):
    lifted = values_in * scales
    summed = None
    for weight, entry in zip(weights, NEIGHBOURS):
        term = weight * shifted(lifted, entry[0], entry[1])
        summed = term if summed is None else summed + term
    return shifted(values_in, 0, 0) - shifted(scales, 0, 0) * summed

def reference(intensity, agreement, basis_block):
    levels = jnp.pad(intensity.astype(jnp.float32), 3)
    counts = jnp.pad(agreement.astype(jnp.float32), ((0, 0), (3, 3), (3, 3)))
    inside = jnp.pad(jnp.ones((NR, NC), jnp.float32), 3)
    weights = neighbour_weights(levels, counts, inside)
    scales = degree_scales(weights)
    inner_weights = [cropped(weight, 2) for weight in weights]
    inner_scales = cropped(scales, 1)

    def apply_group(group):
        padded = jnp.pad(group, ((0, 0), (1, 1), (1, 1)))
        first = apply_once(padded, inner_weights, inner_scales)
        padded = jnp.pad(first, ((0, 0), (1, 1), (1, 1)))
        return apply_once(padded, inner_weights, inner_scales)
    groups = basis_block.reshape(K // 8, 8, NR, NC)
    filtered = lax.map(apply_group, groups).reshape(K, NR * NC)
    gram = jnp.dot(filtered.astype(jnp.float32), filtered.T.astype(jnp.float32), precision=lax.Precision.HIGHEST, preferred_element_type=jnp.float32) / float(NR * NC)
    factor = jnp.linalg.cholesky(gram)
    ortho = jax.scipy.linalg.solve_triangular(factor, filtered, lower=True)
    return (ortho.reshape(K, NR, NC), factor.T)
```

```python
import jax
import jax.numpy as jnp
from jax import lax
from jax.sharding import PartitionSpec as P

INV_SIGMA = 1.0 / 40.0
NEIGHBOURS = (
    (0, 1, 0, 1, 1.0 / 9.0),
    (0, -1, 0, 0, 1.0 / 9.0),
    (1, 0, 1, 1, 1.0 / 9.0),
    (-1, 0, 1, 0, 1.0 / 9.0),
    (1, 1, 2, 1, 1.0 / 18.0),
    (-1, -1, 2, 0, 1.0 / 18.0),
    (1, -1, 3, 1, 1.0 / 18.0),
    (-1, 1, 3, 0, 1.0 / 18.0),
)
AXES = ("row", "col")


def from_neighbour(block, step_row, step_col):
    rows = lax.axis_size("row")
    cols = lax.axis_size("col")
    route = []
    for r in range(rows):
        for c in range(cols):
            tr, tc = r + step_row, c + step_col
            if 0 <= tr < rows and 0 <= tc < cols:
                route.append((r * cols + c, tr * cols + tc))
    return lax.ppermute(block, AXES, route)


def padded(cells, width):
    height = cells.shape[-2]
    span = cells.shape[-1]
    top = cells[..., :width, :]
    bottom = cells[..., height - width :, :]
    left = cells[..., :, :width]
    right = cells[..., :, span - width :]
    top_left = cells[..., :width, :width]
    top_right = cells[..., :width, span - width :]
    bottom_left = cells[..., height - width :, :width]
    bottom_right = cells[..., height - width :, span - width :]
    north = jnp.concatenate(
        [
            from_neighbour(bottom_right, 1, 1),
            from_neighbour(bottom, 1, 0),
            from_neighbour(bottom_left, 1, -1),
        ],
        axis=-1,
    )
    middle = jnp.concatenate(
        [from_neighbour(right, 0, 1), cells, from_neighbour(left, 0, -1)], axis=-1
    )
    south = jnp.concatenate(
        [
            from_neighbour(top_right, -1, 1),
            from_neighbour(top, -1, 0),
            from_neighbour(top_left, -1, -1),
        ],
        axis=-1,
    )
    return jnp.concatenate([north, middle, south], axis=-2)


def shifted(array, step_row, step_col):
    height = array.shape[-2]
    width = array.shape[-1]
    return array[..., 1 + step_row : height - 1 + step_row, 1 + step_col : width - 1 + step_col]


def cropped(array, cycle):
    return array[..., cycle:-cycle, cycle:-cycle]


def neighbour_weights(levels, counts, inside):
    center = shifted(levels, 0, 0)
    center_in = shifted(inside, 0, 0)
    result = []
    for step_row, step_col, channel, at_center, factor in NEIGHBOURS:
        other = shifted(levels, step_row, step_col)
        if at_center == 1:
            source = shifted(counts[channel], 0, 0)
        else:
            source = shifted(counts[channel], step_row, step_col)
        gap = (center - other) * INV_SIGMA
        result.append(
            (1.0 + source)
            * factor
            * jnp.exp(-gap * gap)
            * center_in
            * shifted(inside, step_row, step_col)
        )
    return result


def degree_scales(weights):
    degree = weights[0]
    for weight in weights[1:]:
        degree = degree + weight
    return lax.rsqrt(1.0 + degree)


def apply_once(values_in, weights, scales):
    lifted = values_in * scales
    summed = None
    for weight, entry in zip(weights, NEIGHBOURS):
        term = weight * shifted(lifted, entry[0], entry[1])
        summed = term if summed is None else summed + term
    return shifted(values_in, 0, 0) - shifted(scales, 0, 0) * summed


def per_device(intensity, agreement, basis_block):
    vectors, tile_rows, tile_cols = basis_block.shape
    row_count = lax.axis_size("row")
    col_count = lax.axis_size("col")
    total_rows = tile_rows * row_count
    total_cols = tile_cols * col_count
    labels = jnp.concatenate((intensity[None], agreement), axis=0)
    labels_wide = padded(labels, 3)
    extended = padded(basis_block, 2)
    row_ids = lax.axis_index("row") * tile_rows + jnp.arange(-3, tile_rows + 3, dtype=jnp.int32)
    col_ids = lax.axis_index("col") * tile_cols + jnp.arange(-3, tile_cols + 3, dtype=jnp.int32)
    row_in = ((row_ids >= 0) & (row_ids < total_rows)).astype(jnp.float32)
    col_in = ((col_ids >= 0) & (col_ids < total_cols)).astype(jnp.float32)
    inside = row_in[:, None] * col_in[None, :]
    levels = labels_wide[0].astype(jnp.float32)
    counts = labels_wide[1:].astype(jnp.float32)
    weights = neighbour_weights(levels, counts, inside)
    scales = degree_scales(weights)
    first = apply_once(extended, [cropped(w, 1) for w in weights], scales)
    filtered = apply_once(first, [cropped(w, 2) for w in weights], cropped(scales, 1))
    flat = filtered.reshape(vectors, tile_rows * tile_cols)
    pixel_total = float(total_rows * total_cols)
    gram_local = jnp.dot(
        flat, flat.T, precision=lax.Precision.HIGHEST, preferred_element_type=jnp.float32
    )
    gram = lax.psum(gram_local, AXES) / pixel_total
    factor = jnp.linalg.cholesky(gram)
    ortho = jax.scipy.linalg.solve_triangular(factor, flat, lower=True)
    return (ortho.reshape(vectors, tile_rows, tile_cols), factor.T)


def solution(mesh):
    return jax.shard_map(
        per_device,
        mesh=mesh,
        in_specs=(P("row", "col"), P(None, "row", "col"), P(None, "row", "col")),
        out_specs=(P(None, "row", "col"), P()),
        check_vma=False,
    )
```

```python
import jax
import jax.numpy as jnp
from jax import lax
from jax.sharding import PartitionSpec as P

INV_SIGMA = 1.0 / 40.0
NEIGHBOURS = (
    (0, 1, 0, 1, 1.0 / 9.0),
    (0, -1, 0, 0, 1.0 / 9.0),
    (1, 0, 1, 1, 1.0 / 9.0),
    (-1, 0, 1, 0, 1.0 / 9.0),
    (1, 1, 2, 1, 1.0 / 18.0),
    (-1, -1, 2, 0, 1.0 / 18.0),
    (1, -1, 3, 1, 1.0 / 18.0),
    (-1, 1, 3, 0, 1.0 / 18.0),
)


def padded(cells, sides, width):
    for axis, dim in sides:
        count = lax.axis_size(axis)
        ends = count - 1
        head = lax.slice_in_dim(cells, 0, width, axis=dim)
        tail = lax.slice_in_dim(cells, cells.shape[dim] - width, cells.shape[dim], axis=dim)
        cells = jnp.concatenate(
            [
                lax.ppermute(tail, axis, [(i, (i + 1) % count) for i in range(ends)]),
                cells,
                lax.ppermute(head, axis, [((i + 1) % count, i) for i in range(ends)]),
            ],
            axis=dim,
        )
    return cells


def shifted(array, step_row, step_col):
    height = array.shape[-2]
    width = array.shape[-1]
    return array[..., 1 + step_row : height - 1 + step_row, 1 + step_col : width - 1 + step_col]


def cropped(array, cycle):
    return array[..., cycle:-cycle, cycle:-cycle]


def neighbour_weights(levels, counts, inside):
    center = shifted(levels, 0, 0)
    center_in = shifted(inside, 0, 0)
    result = []
    for step_row, step_col, channel, at_center, factor in NEIGHBOURS:
        other = shifted(levels, step_row, step_col)
        if at_center == 1:
            source = shifted(counts[channel], 0, 0)
        else:
            source = shifted(counts[channel], step_row, step_col)
        gap = (center - other) * INV_SIGMA
        result.append(
            (1.0 + source)
            * factor
            * jnp.exp(-gap * gap)
            * center_in
            * shifted(inside, step_row, step_col)
        )
    return result


def degree_scales(weights):
    degree = weights[0]
    for weight in weights[1:]:
        degree = degree + weight
    return lax.rsqrt(1.0 + degree)


def apply_once(values_in, weights, scales):
    lifted = values_in * scales
    summed = None
    for weight, entry in zip(weights, NEIGHBOURS):
        term = weight * shifted(lifted, entry[0], entry[1])
        summed = term if summed is None else summed + term
    return shifted(values_in, 0, 0) - shifted(scales, 0, 0) * summed


def exchange_sum(block, axis, low_bit, bits):
    count = lax.axis_size(axis)
    received = [block]
    for offset in range(1, 1 << bits):
        flip = offset << low_bit
        route = [(i, i ^ flip) for i in range(count)]
        received.append(lax.ppermute(block, axis, route))
    while len(received) > 1:
        received = [received[i] + received[i + 1] for i in range(0, len(received), 2)]
    return received[0]


def all_sum(block, axis):
    count = lax.axis_size(axis)
    levels = count.bit_length() - 1
    if (1 << levels) != count:
        return lax.psum(block, axis)
    low_bit = 0
    while low_bit < levels:
        bits = min(2, levels - low_bit)
        block = exchange_sum(block, axis, low_bit, bits)
        low_bit += bits
    return block


def per_device(intensity, agreement, basis_block):
    vectors, tile_rows, tile_cols = basis_block.shape
    row_count = lax.axis_size("row")
    col_count = lax.axis_size("col")
    total_rows = tile_rows * row_count
    total_cols = tile_cols * col_count
    labels = jnp.concatenate((intensity[None], agreement), axis=0)
    labels_wide = padded(labels, (("row", 1), ("col", 2)), 3)
    row_ids = lax.axis_index("row") * tile_rows + jnp.arange(-3, tile_rows + 3, dtype=jnp.int32)
    col_ids = lax.axis_index("col") * tile_cols + jnp.arange(-3, tile_cols + 3, dtype=jnp.int32)
    row_in = ((row_ids >= 0) & (row_ids < total_rows)).astype(jnp.float32)
    col_in = ((col_ids >= 0) & (col_ids < total_cols)).astype(jnp.float32)
    inside = row_in[:, None] * col_in[None, :]
    levels = labels_wide[0].astype(jnp.float32)
    counts = labels_wide[1:].astype(jnp.float32)
    weights = neighbour_weights(levels, counts, inside)
    scales = degree_scales(weights)
    cycle_zero = [cropped(weight, 2) for weight in weights]
    filtered = basis_block
    for repeat in range(2):
        extended = padded(filtered, (("row", 1), ("col", 2)), 1)
        filtered = apply_once(extended, cycle_zero, cropped(scales, 1))
    pixel_total = float(total_rows * total_cols)
    gram_local = jnp.einsum(
        "krc,jrc->kj", filtered, filtered,
        precision=lax.Precision.HIGHEST, preferred_element_type=jnp.float32,
    )
    gram = all_sum(all_sum(gram_local, "col"), "row") / pixel_total
    factor = jnp.linalg.cholesky(gram)
    inverse = jax.scipy.linalg.solve_triangular(
        factor, jnp.eye(vectors, dtype=jnp.float32), lower=True
    )
    ortho = jnp.einsum(
        "kj,jrc->krc", inverse, filtered,
        precision=lax.Precision.HIGHEST, preferred_element_type=jnp.float32,
    )
    return (ortho, factor.T)


def solution(mesh):
    return jax.shard_map(
        per_device,
        mesh=mesh,
        in_specs=(P("row", "col"), P(None, "row", "col"), P(None, "row", "col")),
        out_specs=(P(None, "row", "col"), P()),
        check_vma=False,
    )
```

```python
import jax
import jax.numpy as jnp
from jax import lax
from jax.sharding import PartitionSpec as P

INV_SIGMA = 1.0 / 40.0
NEIGHBOURS = (
    (0, 1, 0, 1, 1.0 / 9.0),
    (0, -1, 0, 0, 1.0 / 9.0),
    (1, 0, 1, 1, 1.0 / 9.0),
    (-1, 0, 1, 0, 1.0 / 9.0),
    (1, 1, 2, 1, 1.0 / 18.0),
    (-1, -1, 2, 0, 1.0 / 18.0),
    (1, -1, 3, 1, 1.0 / 18.0),
    (-1, 1, 3, 0, 1.0 / 18.0),
)


def padded(cells, sides, width):
    for axis, dim in sides:
        count = lax.axis_size(axis)
        ends = count - 1
        head = lax.slice_in_dim(cells, 0, width, axis=dim)
        tail = lax.slice_in_dim(cells, cells.shape[dim] - width, cells.shape[dim], axis=dim)
        cells = jnp.concatenate(
            [
                lax.ppermute(tail, axis, [(i, (i + 1) % count) for i in range(ends)]),
                cells,
                lax.ppermute(head, axis, [((i + 1) % count, i) for i in range(ends)]),
            ],
            axis=dim,
        )
    return cells


def shifted(array, step_row, step_col):
    height = array.shape[-2]
    width = array.shape[-1]
    return array[..., 1 + step_row : height - 1 + step_row, 1 + step_col : width - 1 + step_col]


def cropped(array, cycle):
    return array[..., cycle:-cycle, cycle:-cycle]


def neighbour_weights(levels, counts, inside):
    center = shifted(levels, 0, 0)
    center_in = shifted(inside, 0, 0)
    result = []
    for step_row, step_col, channel, at_center, factor in NEIGHBOURS:
        other = shifted(levels, step_row, step_col)
        if at_center == 1:
            source = shifted(counts[channel], 0, 0)
        else:
            source = shifted(counts[channel], step_row, step_col)
        gap = (center - other) * INV_SIGMA
        result.append(
            (1.0 + source)
            * factor
            * jnp.exp(-gap * gap)
            * center_in
            * shifted(inside, step_row, step_col)
        )
    return result


def degree_scales(weights):
    degree = weights[0]
    for weight in weights[1:]:
        degree = degree + weight
    return lax.rsqrt(1.0 + degree)


def apply_once(values_in, weights, scales):
    lifted = values_in * scales
    summed = None
    for weight, entry in zip(weights, NEIGHBOURS):
        term = weight * shifted(lifted, entry[0], entry[1])
        summed = term if summed is None else summed + term
    return shifted(values_in, 0, 0) - shifted(scales, 0, 0) * summed


def shifted_pixels(array, step_row, step_col):
    height = array.shape[0]
    width = array.shape[1]
    return array[1 + step_row : height - 1 + step_row, 1 + step_col : width - 1 + step_col]


def apply_pixels(values_in, weights, scales):
    lifted = values_in * scales[:, :, None]
    summed = None
    for weight, entry in zip(weights, NEIGHBOURS):
        term = weight[:, :, None] * shifted_pixels(lifted, entry[0], entry[1])
        summed = term if summed is None else summed + term
    return shifted_pixels(values_in, 0, 0) - shifted(scales, 0, 0)[:, :, None] * summed


def exchange_sum(block, axis, low_bit, bits):
    count = lax.axis_size(axis)
    received = [block]
    for offset in range(1, 1 << bits):
        flip = offset << low_bit
        route = [(i, i ^ flip) for i in range(count)]
        received.append(lax.ppermute(block, axis, route))
    while len(received) > 1:
        received = [received[i] + received[i + 1] for i in range(0, len(received), 2)]
    return received[0]


def all_sum(block, axis):
    count = lax.axis_size(axis)
    levels = count.bit_length() - 1
    if (1 << levels) != count:
        return lax.psum(block, axis)
    low_bit = 0
    while low_bit < levels:
        bits = min(2, levels - low_bit)
        block = exchange_sum(block, axis, low_bit, bits)
        low_bit += bits
    return block


def per_device(intensity, agreement, basis_block):
    vectors, tile_rows, tile_cols = basis_block.shape
    row_count = lax.axis_size("row")
    col_count = lax.axis_size("col")
    total_rows = tile_rows * row_count
    total_cols = tile_cols * col_count
    labels = jnp.concatenate((intensity[None], agreement), axis=0)
    labels_wide = padded(labels, (("row", 1), ("col", 2)), 3)
    row_ids = lax.axis_index("row") * tile_rows + jnp.arange(-3, tile_rows + 3, dtype=jnp.int32)
    col_ids = lax.axis_index("col") * tile_cols + jnp.arange(-3, tile_cols + 3, dtype=jnp.int32)
    row_in = ((row_ids >= 0) & (row_ids < total_rows)).astype(jnp.float32)
    col_in = ((col_ids >= 0) & (col_ids < total_cols)).astype(jnp.float32)
    inside = row_in[:, None] * col_in[None, :]
    levels = labels_wide[0].astype(jnp.float32)
    counts = labels_wide[1:].astype(jnp.float32)
    weights = neighbour_weights(levels, counts, inside)
    scales = degree_scales(weights)
    pixels = jnp.transpose(basis_block, (1, 2, 0))
    extended = padded(pixels, (("row", 0), ("col", 1)), 2)
    first = apply_pixels(extended, [cropped(weight, 1) for weight in weights], scales)
    filtered = apply_pixels(first, [cropped(weight, 2) for weight in weights], cropped(scales, 1))
    pixel_total = float(total_rows * total_cols)
    gram_local = jnp.einsum(
        "rck,rcj->kj", filtered, filtered,
        precision=lax.Precision.HIGHEST, preferred_element_type=jnp.float32,
    )
    gram = all_sum(all_sum(gram_local, "col"), "row") / pixel_total
    factor = jnp.linalg.cholesky(gram)
    inverse = jax.scipy.linalg.solve_triangular(
        factor, jnp.eye(vectors, dtype=jnp.float32), lower=True
    )
    ortho = jnp.einsum(
        "kj,rcj->krc", inverse, filtered,
        precision=lax.Precision.HIGHEST, preferred_element_type=jnp.float32,
    )
    return (ortho, factor.T)


def solution(mesh):
    return jax.shard_map(
        per_device,
        mesh=mesh,
        in_specs=(P("row", "col"), P(None, "row", "col"), P(None, "row", "col")),
        out_specs=(P(None, "row", "col"), P()),
        check_vma=False,
    )
```

```python
import jax
import jax.numpy as jnp
from jax import lax
from jax.sharding import PartitionSpec as P

INV_SIGMA = 1.0 / 40.0
NEIGHBOURS = (
    (0, 1, 0, 1, 1.0 / 9.0),
    (0, -1, 0, 0, 1.0 / 9.0),
    (1, 0, 1, 1, 1.0 / 9.0),
    (-1, 0, 1, 0, 1.0 / 9.0),
    (1, 1, 2, 1, 1.0 / 18.0),
    (-1, -1, 2, 0, 1.0 / 18.0),
    (1, -1, 3, 1, 1.0 / 18.0),
    (-1, 1, 3, 0, 1.0 / 18.0),
)


def padded(cells, sides, width):
    for axis, dim in sides:
        count = lax.axis_size(axis)
        ends = count - 1
        head = lax.slice_in_dim(cells, 0, width, axis=dim)
        tail = lax.slice_in_dim(cells, cells.shape[dim] - width, cells.shape[dim], axis=dim)
        cells = jnp.concatenate(
            [
                lax.ppermute(tail, axis, [(i, (i + 1) % count) for i in range(ends)]),
                cells,
                lax.ppermute(head, axis, [((i + 1) % count, i) for i in range(ends)]),
            ],
            axis=dim,
        )
    return cells


def shifted(array, step_row, step_col):
    height = array.shape[-2]
    width = array.shape[-1]
    return array[..., 1 + step_row : height - 1 + step_row, 1 + step_col : width - 1 + step_col]


def cropped(array, cycle):
    return array[..., cycle:-cycle, cycle:-cycle]


def neighbour_weights(levels, counts, inside):
    center = shifted(levels, 0, 0)
    center_in = shifted(inside, 0, 0)
    result = []
    for step_row, step_col, channel, at_center, factor in NEIGHBOURS:
        other = shifted(levels, step_row, step_col)
        if at_center == 1:
            source = shifted(counts[channel], 0, 0)
        else:
            source = shifted(counts[channel], step_row, step_col)
        gap = (center - other) * INV_SIGMA
        result.append(
            (1.0 + source)
            * factor
            * jnp.exp(-gap * gap)
            * center_in
            * shifted(inside, step_row, step_col)
        )
    return result


def degree_scales(weights):
    degree = weights[0]
    for weight in weights[1:]:
        degree = degree + weight
    return lax.rsqrt(1.0 + degree)


def apply_once(values_in, weights, scales):
    lifted = values_in * scales
    summed = None
    for weight, entry in zip(weights, NEIGHBOURS):
        term = weight * shifted(lifted, entry[0], entry[1])
        summed = term if summed is None else summed + term
    return shifted(values_in, 0, 0) - shifted(scales, 0, 0) * summed


def shifted_pixels(array, step_row, step_col):
    height = array.shape[0]
    width = array.shape[1]
    return array[1 + step_row : height - 1 + step_row, 1 + step_col : width - 1 + step_col]


def apply_pixels(values_in, weights, scales):
    lifted = values_in * scales[:, :, None]
    summed = None
    for weight, entry in zip(weights, NEIGHBOURS):
        term = weight[:, :, None] * shifted_pixels(lifted, entry[0], entry[1])
        summed = term if summed is None else summed + term
    return shifted_pixels(values_in, 0, 0) - shifted(scales, 0, 0)[:, :, None] * summed


def exchange_sum(block, axis, low_bit, bits):
    count = lax.axis_size(axis)
    received = [block]
    for offset in range(1, 1 << bits):
        flip = offset << low_bit
        route = [(i, i ^ flip) for i in range(count)]
        received.append(lax.ppermute(block, axis, route))
    while len(received) > 1:
        received = [received[i] + received[i + 1] for i in range(0, len(received), 2)]
    return received[0]


def all_sum(block, axis):
    count = lax.axis_size(axis)
    levels = count.bit_length() - 1
    if (1 << levels) != count:
        return lax.psum(block, axis)
    low_bit = 0
    while low_bit < levels:
        bits = min(2, levels - low_bit)
        block = exchange_sum(block, axis, low_bit, bits)
        low_bit += bits
    return block


def per_device(intensity, agreement, basis_block):
    vectors, tile_rows, tile_cols = basis_block.shape
    row_count = lax.axis_size("row")
    col_count = lax.axis_size("col")
    total_rows = tile_rows * row_count
    total_cols = tile_cols * col_count
    labels = jnp.concatenate((intensity[None], agreement), axis=0)
    labels_wide = padded(labels, (("row", 1), ("col", 2)), 3)
    row_ids = lax.axis_index("row") * tile_rows + jnp.arange(-3, tile_rows + 3, dtype=jnp.int32)
    col_ids = lax.axis_index("col") * tile_cols + jnp.arange(-3, tile_cols + 3, dtype=jnp.int32)
    row_in = ((row_ids >= 0) & (row_ids < total_rows)).astype(jnp.float32)
    col_in = ((col_ids >= 0) & (col_ids < total_cols)).astype(jnp.float32)
    inside = row_in[:, None] * col_in[None, :]
    levels = labels_wide[0].astype(jnp.float32)
    counts = labels_wide[1:].astype(jnp.float32)
    weights = neighbour_weights(levels, counts, inside)
    scales = degree_scales(weights)
    pixels = jnp.transpose(basis_block, (1, 2, 0))
    extended = padded(pixels, (("row", 0), ("col", 1)), 2)
    stacked = jnp.stack(weights)
    ring_weights = cropped(stacked, 1)
    tile_weights = cropped(stacked, 2)
    first = apply_pixels(extended, [ring_weights[i] for i in range(len(weights))], scales)
    filtered = apply_pixels(first, [tile_weights[i] for i in range(len(weights))], cropped(scales, 1))
    pixel_total = float(total_rows * total_cols)
    gram_local = jnp.einsum(
        "rck,rcj->kj", filtered, filtered,
        precision=lax.Precision.HIGHEST, preferred_element_type=jnp.float32,
    )
    gram = all_sum(all_sum(gram_local, "col"), "row") / pixel_total
    factor = jnp.linalg.cholesky(gram)
    inverse = jax.scipy.linalg.solve_triangular(
        factor, jnp.eye(vectors, dtype=jnp.float32), lower=True
    )
    ortho = jnp.einsum(
        "kj,rcj->krc", inverse, filtered,
        precision=lax.Precision.HIGHEST, preferred_element_type=jnp.float32,
    )
    return (ortho, factor.T)


def solution(mesh):
    return jax.shard_map(
        per_device,
        mesh=mesh,
        in_specs=(P("row", "col"), P(None, "row", "col"), P(None, "row", "col")),
        out_specs=(P(None, "row", "col"), P()),
        check_vma=False,
    )
```

```python
import jax
import jax.numpy as jnp
from jax import lax
from jax.experimental import pallas as pl
from jax.experimental.pallas import tpu as pltpu
from jax.sharding import PartitionSpec as P

INV_SIGMA = 1.0 / 40.0
NEIGHBOURS = (
    (0, 1, 0, 1, 1.0 / 9.0),
    (0, -1, 0, 0, 1.0 / 9.0),
    (1, 0, 1, 1, 1.0 / 9.0),
    (-1, 0, 1, 0, 1.0 / 9.0),
    (1, 1, 2, 1, 1.0 / 18.0),
    (-1, -1, 2, 0, 1.0 / 18.0),
    (1, -1, 3, 1, 1.0 / 18.0),
    (-1, 1, 3, 0, 1.0 / 18.0),
)


def padded(cells, sides, width):
    for axis, dim in sides:
        count = lax.axis_size(axis)
        ends = count - 1
        head = lax.slice_in_dim(cells, 0, width, axis=dim)
        tail = lax.slice_in_dim(cells, cells.shape[dim] - width, cells.shape[dim], axis=dim)
        cells = jnp.concatenate(
            [
                lax.ppermute(tail, axis, [(i, (i + 1) % count) for i in range(ends)]),
                cells,
                lax.ppermute(head, axis, [((i + 1) % count, i) for i in range(ends)]),
            ],
            axis=dim,
        )
    return cells


def shifted(array, step_row, step_col):
    height = array.shape[-2]
    width = array.shape[-1]
    return array[..., 1 + step_row : height - 1 + step_row, 1 + step_col : width - 1 + step_col]


def cropped(array, cycle):
    return array[..., cycle:-cycle, cycle:-cycle]


def neighbour_weights(levels, counts, inside):
    center = shifted(levels, 0, 0)
    center_in = shifted(inside, 0, 0)
    result = []
    for step_row, step_col, channel, at_center, factor in NEIGHBOURS:
        other = shifted(levels, step_row, step_col)
        if at_center == 1:
            source = shifted(counts[channel], 0, 0)
        else:
            source = shifted(counts[channel], step_row, step_col)
        gap = (center - other) * INV_SIGMA
        result.append(
            (1.0 + source)
            * factor
            * jnp.exp(-gap * gap)
            * center_in
            * shifted(inside, step_row, step_col)
        )
    return result


def degree_scales(weights):
    degree = weights[0]
    for weight in weights[1:]:
        degree = degree + weight
    return lax.rsqrt(1.0 + degree)


def apply_once(values_in, weights, scales):
    lifted = values_in * scales
    summed = None
    for weight, entry in zip(weights, NEIGHBOURS):
        term = weight * shifted(lifted, entry[0], entry[1])
        summed = term if summed is None else summed + term
    return shifted(values_in, 0, 0) - shifted(scales, 0, 0) * summed


def shifted_pixels(array, step_row, step_col):
    height = array.shape[0]
    width = array.shape[1]
    return array[1 + step_row : height - 1 + step_row, 1 + step_col : width - 1 + step_col]


def apply_pixels(values_in, weights, scales):
    lifted = values_in * scales[:, :, None]
    summed = None
    for weight, entry in zip(weights, NEIGHBOURS):
        term = weight[:, :, None] * shifted_pixels(lifted, entry[0], entry[1])
        summed = term if summed is None else summed + term
    return shifted_pixels(values_in, 0, 0) - shifted(scales, 0, 0)[:, :, None] * summed


def exchange_sum(block, axis, low_bit, bits):
    count = lax.axis_size(axis)
    received = [block]
    for offset in range(1, 1 << bits):
        flip = offset << low_bit
        route = [(i, i ^ flip) for i in range(count)]
        received.append(lax.ppermute(block, axis, route))
    while len(received) > 1:
        received = [received[i] + received[i + 1] for i in range(0, len(received), 2)]
    return received[0]


def all_sum(block, axis):
    count = lax.axis_size(axis)
    levels = count.bit_length() - 1
    if (1 << levels) != count:
        return lax.psum(block, axis)
    low_bit = 0
    while low_bit < levels:
        bits = min(2, levels - low_bit)
        block = exchange_sum(block, axis, low_bit, bits)
        low_bit += bits
    return block


def factor_kernel(gram_ref, upper_ref, inverse_ref, work_ref):
    size = gram_ref.shape[0]
    work_ref[...] = gram_ref[...]
    sub = lax.broadcasted_iota(jnp.int32, (size, size), 0)
    lane = lax.broadcasted_iota(jnp.int32, (size, size), 1)
    upper_ref[...] = jnp.zeros((size, size), jnp.float32)
    inverse_ref[...] = jnp.where(sub == lane, 1.0, 0.0).astype(jnp.float32)
    lane_row = lax.broadcasted_iota(jnp.int32, (1, size), 1)
    sub_col = lax.broadcasted_iota(jnp.int32, (size, 1), 0)

    def step(j, carry):
        row = work_ref[pl.ds(j, 1), :]
        pivot = jnp.sum(jnp.where(lane_row == j, row, 0.0), axis=1, keepdims=True)
        root = jnp.sqrt(pivot)
        urow = jnp.where(lane_row >= j, row / root, 0.0)
        column = jnp.transpose(jnp.broadcast_to(row, (8, size)))[:, :1]
        lcol = jnp.where(sub_col >= j, column / root, 0.0)
        work_ref[...] = work_ref[...] - lcol * urow
        upper_ref[pl.ds(j, 1), :] = urow
        brow = inverse_ref[pl.ds(j, 1), :] / root
        below = jnp.where(sub_col > j, lcol, 0.0)
        inverse_ref[...] = inverse_ref[...] - below * brow
        inverse_ref[pl.ds(j, 1), :] = brow
        return carry

    lax.fori_loop(0, size, step, 0)


def factor_and_inverse(gram):
    size = gram.shape[0]
    return pl.pallas_call(
        factor_kernel,
        out_shape=(jax.ShapeDtypeStruct((size, size), jnp.float32),) * 2,
        scratch_shapes=[pltpu.VMEM((size, size), jnp.float32)],
    )(gram)


def per_device(intensity, agreement, basis_block):
    vectors, tile_rows, tile_cols = basis_block.shape
    row_count = lax.axis_size("row")
    col_count = lax.axis_size("col")
    total_rows = tile_rows * row_count
    total_cols = tile_cols * col_count
    labels = jnp.concatenate((intensity[None], agreement), axis=0)
    labels_wide = padded(labels, (("row", 1), ("col", 2)), 3)
    row_ids = lax.axis_index("row") * tile_rows + jnp.arange(-3, tile_rows + 3, dtype=jnp.int32)
    col_ids = lax.axis_index("col") * tile_cols + jnp.arange(-3, tile_cols + 3, dtype=jnp.int32)
    row_in = ((row_ids >= 0) & (row_ids < total_rows)).astype(jnp.float32)
    col_in = ((col_ids >= 0) & (col_ids < total_cols)).astype(jnp.float32)
    inside = row_in[:, None] * col_in[None, :]
    levels = labels_wide[0].astype(jnp.float32)
    counts = labels_wide[1:].astype(jnp.float32)
    weights = neighbour_weights(levels, counts, inside)
    scales = degree_scales(weights)
    pixels = jnp.transpose(basis_block, (1, 2, 0))
    extended = padded(pixels, (("row", 0), ("col", 1)), 2)
    stacked = jnp.stack(weights)
    ring_weights = cropped(stacked, 1)
    tile_weights = cropped(stacked, 2)
    first = apply_pixels(extended, [ring_weights[i] for i in range(len(weights))], scales)
    filtered = apply_pixels(first, [tile_weights[i] for i in range(len(weights))], cropped(scales, 1))
    pixel_total = float(total_rows * total_cols)
    gram_local = jnp.einsum(
        "rck,rcj->kj", filtered, filtered,
        precision=lax.Precision.HIGHEST, preferred_element_type=jnp.float32,
    )
    gram = all_sum(all_sum(gram_local, "col"), "row") / pixel_total
    upper, inverse = factor_and_inverse(gram)
    ortho = jnp.einsum(
        "kj,rcj->krc", inverse, filtered,
        precision=lax.Precision.HIGHEST, preferred_element_type=jnp.float32,
    )
    return (ortho, upper)


def solution(mesh):
    return jax.shard_map(
        per_device,
        mesh=mesh,
        in_specs=(P("row", "col"), P(None, "row", "col"), P(None, "row", "col")),
        out_specs=(P(None, "row", "col"), P()),
        check_vma=False,
    )
```

```python
import jax
import jax.numpy as jnp
from jax import lax
from jax.sharding import PartitionSpec as P

INV_SIGMA = 1.0 / 40.0
NEIGHBOURS = (
    (0, 1, 0, 1, 1.0 / 9.0),
    (0, -1, 0, 0, 1.0 / 9.0),
    (1, 0, 1, 1, 1.0 / 9.0),
    (-1, 0, 1, 0, 1.0 / 9.0),
    (1, 1, 2, 1, 1.0 / 18.0),
    (-1, -1, 2, 0, 1.0 / 18.0),
    (1, -1, 3, 1, 1.0 / 18.0),
    (-1, 1, 3, 0, 1.0 / 18.0),
)


def padded(cells, sides, width):
    for axis, dim in sides:
        count = lax.axis_size(axis)
        ends = count - 1
        head = lax.slice_in_dim(cells, 0, width, axis=dim)
        tail = lax.slice_in_dim(cells, cells.shape[dim] - width, cells.shape[dim], axis=dim)
        cells = jnp.concatenate(
            [
                lax.ppermute(tail, axis, [(i, (i + 1) % count) for i in range(ends)]),
                cells,
                lax.ppermute(head, axis, [((i + 1) % count, i) for i in range(ends)]),
            ],
            axis=dim,
        )
    return cells


def shifted(array, step_row, step_col):
    height = array.shape[-2]
    width = array.shape[-1]
    return array[..., 1 + step_row : height - 1 + step_row, 1 + step_col : width - 1 + step_col]


def cropped(array, cycle):
    return array[..., cycle:-cycle, cycle:-cycle]


def neighbour_weights(levels, counts, inside):
    center = shifted(levels, 0, 0)
    center_in = shifted(inside, 0, 0)
    result = []
    for step_row, step_col, channel, at_center, factor in NEIGHBOURS:
        other = shifted(levels, step_row, step_col)
        if at_center == 1:
            source = shifted(counts[channel], 0, 0)
        else:
            source = shifted(counts[channel], step_row, step_col)
        gap = (center - other) * INV_SIGMA
        result.append(
            (1.0 + source)
            * factor
            * jnp.exp(-gap * gap)
            * center_in
            * shifted(inside, step_row, step_col)
        )
    return result


def degree_scales(weights):
    degree = weights[0]
    for weight in weights[1:]:
        degree = degree + weight
    return lax.rsqrt(1.0 + degree)


def apply_once(values_in, weights, scales):
    lifted = values_in * scales
    summed = None
    for weight, entry in zip(weights, NEIGHBOURS):
        term = weight * shifted(lifted, entry[0], entry[1])
        summed = term if summed is None else summed + term
    return shifted(values_in, 0, 0) - shifted(scales, 0, 0) * summed


def shifted_pixels(array, step_row, step_col):
    height = array.shape[0]
    width = array.shape[1]
    return array[1 + step_row : height - 1 + step_row, 1 + step_col : width - 1 + step_col]


def apply_pixels(values_in, weights, scales):
    lifted = values_in * scales[:, :, None]
    summed = None
    for weight, entry in zip(weights, NEIGHBOURS):
        term = weight[:, :, None] * shifted_pixels(lifted, entry[0], entry[1])
        summed = term if summed is None else summed + term
    return shifted_pixels(values_in, 0, 0) - shifted(scales, 0, 0)[:, :, None] * summed


def exchange_sum(block, axis, low_bit, bits):
    count = lax.axis_size(axis)
    received = [block]
    for offset in range(1, 1 << bits):
        flip = offset << low_bit
        route = [(i, i ^ flip) for i in range(count)]
        received.append(lax.ppermute(block, axis, route))
    while len(received) > 1:
        received = [received[i] + received[i + 1] for i in range(0, len(received), 2)]
    return received[0]


def all_sum(block, axis):
    count = lax.axis_size(axis)
    levels = count.bit_length() - 1
    if (1 << levels) != count:
        return lax.psum(block, axis)
    low_bit = 0
    while low_bit < levels:
        bits = min(2, levels - low_bit)
        block = exchange_sum(block, axis, low_bit, bits)
        low_bit += bits
    return block


def per_device(intensity, agreement, basis_block):
    vectors, tile_rows, tile_cols = basis_block.shape
    row_count = lax.axis_size("row")
    col_count = lax.axis_size("col")
    total_rows = tile_rows * row_count
    total_cols = tile_cols * col_count
    labels = jnp.concatenate((intensity[None], agreement), axis=0)
    labels_wide = padded(labels, (("row", 1), ("col", 2)), 3)
    row_ids = lax.axis_index("row") * tile_rows + jnp.arange(-3, tile_rows + 3, dtype=jnp.int32)
    col_ids = lax.axis_index("col") * tile_cols + jnp.arange(-3, tile_cols + 3, dtype=jnp.int32)
    row_in = ((row_ids >= 0) & (row_ids < total_rows)).astype(jnp.float32)
    col_in = ((col_ids >= 0) & (col_ids < total_cols)).astype(jnp.float32)
    inside = row_in[:, None] * col_in[None, :]
    levels = labels_wide[0].astype(jnp.float32)
    counts = labels_wide[1:].astype(jnp.float32)
    weights = neighbour_weights(levels, counts, inside)
    scales = degree_scales(weights)
    pixels = jnp.transpose(basis_block, (1, 2, 0))
    extended = padded(pixels, (("row", 0), ("col", 1)), 2)
    stacked = jnp.stack(weights)
    ring_weights = cropped(stacked, 1)
    tile_weights = cropped(stacked, 2)
    first = apply_pixels(extended, [ring_weights[i] for i in range(len(weights))], scales)
    filtered = apply_pixels(first, [tile_weights[i] for i in range(len(weights))], cropped(scales, 1))
    pixel_total = float(total_rows * total_cols)
    gram_local = jnp.einsum(
        "rck,rcj->kj", filtered, filtered,
        precision=lax.Precision.HIGH, preferred_element_type=jnp.float32,
    )
    gram = all_sum(all_sum(gram_local, "col"), "row") / pixel_total
    factor = jnp.linalg.cholesky(gram)
    inverse = jax.scipy.linalg.solve_triangular(
        factor, jnp.eye(vectors, dtype=jnp.float32), lower=True
    )
    ortho = jnp.einsum(
        "kj,rcj->krc", inverse, filtered,
        precision=lax.Precision.HIGH, preferred_element_type=jnp.float32,
    )
    return (ortho, factor.T)


def solution(mesh):
    return jax.shard_map(
        per_device,
        mesh=mesh,
        in_specs=(P("row", "col"), P(None, "row", "col"), P(None, "row", "col")),
        out_specs=(P(None, "row", "col"), P()),
        check_vma=False,
    )
```

```python
import jax
import jax.numpy as jnp
from jax import lax
from jax.sharding import PartitionSpec as P

INV_SIGMA = 1.0 / 40.0
NEIGHBOURS = (
    (0, 1, 0, 1, 1.0 / 9.0),
    (0, -1, 0, 0, 1.0 / 9.0),
    (1, 0, 1, 1, 1.0 / 9.0),
    (-1, 0, 1, 0, 1.0 / 9.0),
    (1, 1, 2, 1, 1.0 / 18.0),
    (-1, -1, 2, 0, 1.0 / 18.0),
    (1, -1, 3, 1, 1.0 / 18.0),
    (-1, 1, 3, 0, 1.0 / 18.0),
)


def padded(cells, sides, width):
    for axis, dim in sides:
        count = lax.axis_size(axis)
        ends = count - 1
        head = lax.slice_in_dim(cells, 0, width, axis=dim)
        tail = lax.slice_in_dim(cells, cells.shape[dim] - width, cells.shape[dim], axis=dim)
        cells = jnp.concatenate(
            [
                lax.ppermute(tail, axis, [(i, (i + 1) % count) for i in range(ends)]),
                cells,
                lax.ppermute(head, axis, [((i + 1) % count, i) for i in range(ends)]),
            ],
            axis=dim,
        )
    return cells


def shifted(array, step_row, step_col):
    height = array.shape[-2]
    width = array.shape[-1]
    return array[..., 1 + step_row : height - 1 + step_row, 1 + step_col : width - 1 + step_col]


def cropped(array, cycle):
    return array[..., cycle:-cycle, cycle:-cycle]


def neighbour_weights(levels, counts, inside):
    center = shifted(levels, 0, 0)
    center_in = shifted(inside, 0, 0)
    result = []
    for step_row, step_col, channel, at_center, factor in NEIGHBOURS:
        other = shifted(levels, step_row, step_col)
        if at_center == 1:
            source = shifted(counts[channel], 0, 0)
        else:
            source = shifted(counts[channel], step_row, step_col)
        gap = (center - other) * INV_SIGMA
        result.append(
            (1.0 + source)
            * factor
            * jnp.exp(-gap * gap)
            * center_in
            * shifted(inside, step_row, step_col)
        )
    return result


def degree_scales(weights):
    degree = weights[0]
    for weight in weights[1:]:
        degree = degree + weight
    return lax.rsqrt(1.0 + degree)


def apply_once(values_in, weights, scales):
    lifted = values_in * scales
    summed = None
    for weight, entry in zip(weights, NEIGHBOURS):
        term = weight * shifted(lifted, entry[0], entry[1])
        summed = term if summed is None else summed + term
    return shifted(values_in, 0, 0) - shifted(scales, 0, 0) * summed


def shifted_pixels(array, step_row, step_col):
    height = array.shape[0]
    width = array.shape[1]
    return array[1 + step_row : height - 1 + step_row, 1 + step_col : width - 1 + step_col]


def pass_coefficients(weights, scales):
    center = shifted(scales, 0, 0)
    return jnp.stack(
        [center * weight * shifted(scales, entry[0], entry[1]) for weight, entry in zip(weights, NEIGHBOURS)]
    )


def apply_pixels(values_in, coefficients):
    summed = None
    for index, entry in enumerate(NEIGHBOURS):
        term = coefficients[index][:, :, None] * shifted_pixels(values_in, entry[0], entry[1])
        summed = term if summed is None else summed + term
    return shifted_pixels(values_in, 0, 0) - summed


def exchange_sum(block, axis, low_bit, bits):
    count = lax.axis_size(axis)
    received = [block]
    for offset in range(1, 1 << bits):
        flip = offset << low_bit
        route = [(i, i ^ flip) for i in range(count)]
        received.append(lax.ppermute(block, axis, route))
    while len(received) > 1:
        received = [received[i] + received[i + 1] for i in range(0, len(received), 2)]
    return received[0]


def all_sum(block, axis):
    count = lax.axis_size(axis)
    levels = count.bit_length() - 1
    if (1 << levels) != count:
        return lax.psum(block, axis)
    low_bit = 0
    while low_bit < levels:
        bits = min(2, levels - low_bit)
        block = exchange_sum(block, axis, low_bit, bits)
        low_bit += bits
    return block


def per_device(intensity, agreement, basis_block):
    vectors, tile_rows, tile_cols = basis_block.shape
    row_count = lax.axis_size("row")
    col_count = lax.axis_size("col")
    total_rows = tile_rows * row_count
    total_cols = tile_cols * col_count
    labels = jnp.concatenate((intensity[None], agreement), axis=0)
    labels_wide = padded(labels, (("row", 1), ("col", 2)), 3)
    row_ids = lax.axis_index("row") * tile_rows + jnp.arange(-3, tile_rows + 3, dtype=jnp.int32)
    col_ids = lax.axis_index("col") * tile_cols + jnp.arange(-3, tile_cols + 3, dtype=jnp.int32)
    row_in = ((row_ids >= 0) & (row_ids < total_rows)).astype(jnp.float32)
    col_in = ((col_ids >= 0) & (col_ids < total_cols)).astype(jnp.float32)
    inside = row_in[:, None] * col_in[None, :]
    levels = labels_wide[0].astype(jnp.float32)
    counts = labels_wide[1:].astype(jnp.float32)
    weights = neighbour_weights(levels, counts, inside)
    scales = degree_scales(weights)
    pixels = jnp.transpose(basis_block, (1, 2, 0))
    extended = padded(pixels, (("row", 0), ("col", 1)), 2)
    first = apply_pixels(extended, pass_coefficients([cropped(w, 1) for w in weights], scales))
    tile_scales = cropped(scales, 1)
    filtered = apply_pixels(first, pass_coefficients([cropped(w, 2) for w in weights], tile_scales))
    pixel_total = float(total_rows * total_cols)
    gram_local = jnp.einsum(
        "rck,rcj->kj", filtered, filtered,
        precision=lax.Precision.HIGH, preferred_element_type=jnp.float32,
    )
    gram = all_sum(all_sum(gram_local, "col"), "row") / pixel_total
    factor = jnp.linalg.cholesky(gram)
    inverse = jax.scipy.linalg.solve_triangular(
        factor, jnp.eye(vectors, dtype=jnp.float32), lower=True
    )
    ortho = jnp.einsum(
        "kj,rcj->krc", inverse, filtered,
        precision=lax.Precision.HIGH, preferred_element_type=jnp.float32,
    )
    return (ortho, factor.T)


def solution(mesh):
    return jax.shard_map(
        per_device,
        mesh=mesh,
        in_specs=(P("row", "col"), P(None, "row", "col"), P(None, "row", "col")),
        out_specs=(P(None, "row", "col"), P()),
        check_vma=False,
    )
```

```python
import jax
import jax.numpy as jnp
from jax import lax
from jax.sharding import PartitionSpec as P

INV_SIGMA = 1.0 / 40.0
NEIGHBOURS = (
    (0, 1, 0, 1, 1.0 / 9.0),
    (0, -1, 0, 0, 1.0 / 9.0),
    (1, 0, 1, 1, 1.0 / 9.0),
    (-1, 0, 1, 0, 1.0 / 9.0),
    (1, 1, 2, 1, 1.0 / 18.0),
    (-1, -1, 2, 0, 1.0 / 18.0),
    (1, -1, 3, 1, 1.0 / 18.0),
    (-1, 1, 3, 0, 1.0 / 18.0),
)


def padded(cells, sides, width):
    for axis, dim in sides:
        count = lax.axis_size(axis)
        ends = count - 1
        head = lax.slice_in_dim(cells, 0, width, axis=dim)
        tail = lax.slice_in_dim(cells, cells.shape[dim] - width, cells.shape[dim], axis=dim)
        cells = jnp.concatenate(
            [
                lax.ppermute(tail, axis, [(i, (i + 1) % count) for i in range(ends)]),
                cells,
                lax.ppermute(head, axis, [((i + 1) % count, i) for i in range(ends)]),
            ],
            axis=dim,
        )
    return cells


def shifted(array, step_row, step_col):
    height = array.shape[-2]
    width = array.shape[-1]
    return array[..., 1 + step_row : height - 1 + step_row, 1 + step_col : width - 1 + step_col]


def cropped(array, cycle):
    return array[..., cycle:-cycle, cycle:-cycle]


def neighbour_weights(levels, counts, inside):
    center = shifted(levels, 0, 0)
    center_in = shifted(inside, 0, 0)
    result = []
    for step_row, step_col, channel, at_center, factor in NEIGHBOURS:
        other = shifted(levels, step_row, step_col)
        if at_center == 1:
            source = shifted(counts[channel], 0, 0)
        else:
            source = shifted(counts[channel], step_row, step_col)
        gap = (center - other) * INV_SIGMA
        result.append(
            (1.0 + source)
            * factor
            * jnp.exp(-gap * gap)
            * center_in
            * shifted(inside, step_row, step_col)
        )
    return result


def degree_scales(weights):
    degree = weights[0]
    for weight in weights[1:]:
        degree = degree + weight
    return lax.rsqrt(1.0 + degree)


def apply_once(values_in, weights, scales):
    lifted = values_in * scales
    summed = None
    for weight, entry in zip(weights, NEIGHBOURS):
        term = weight * shifted(lifted, entry[0], entry[1])
        summed = term if summed is None else summed + term
    return shifted(values_in, 0, 0) - shifted(scales, 0, 0) * summed


def shifted_pixels(array, step_row, step_col):
    height = array.shape[0]
    width = array.shape[1]
    return array[1 + step_row : height - 1 + step_row, 1 + step_col : width - 1 + step_col]


def pass_coefficients(weights, scales):
    center = shifted(scales, 0, 0)
    return jnp.stack(
        [center * weight * shifted(scales, entry[0], entry[1]) for weight, entry in zip(weights, NEIGHBOURS)]
    )


def apply_pixels(values_in, coefficients):
    summed = None
    for index, entry in enumerate(NEIGHBOURS):
        term = coefficients[index][:, :, None] * shifted_pixels(values_in, entry[0], entry[1])
        summed = term if summed is None else summed + term
    return shifted_pixels(values_in, 0, 0) - summed


def exchange_sum(block, axis, low_bit, bits):
    count = lax.axis_size(axis)
    received = [block]
    for offset in range(1, 1 << bits):
        flip = offset << low_bit
        route = [(i, i ^ flip) for i in range(count)]
        received.append(lax.ppermute(block, axis, route))
    while len(received) > 1:
        received = [received[i] + received[i + 1] for i in range(0, len(received), 2)]
    return received[0]


def all_sum(block, axis):
    count = lax.axis_size(axis)
    levels = count.bit_length() - 1
    if (1 << levels) != count:
        return lax.psum(block, axis)
    low_bit = 0
    while low_bit < levels:
        bits = min(2, levels - low_bit)
        block = exchange_sum(block, axis, low_bit, bits)
        low_bit += bits
    return block


def per_device(intensity, agreement, basis_block):
    vectors, tile_rows, tile_cols = basis_block.shape
    row_count = lax.axis_size("row")
    col_count = lax.axis_size("col")
    total_rows = tile_rows * row_count
    total_cols = tile_cols * col_count
    labels = jnp.concatenate((intensity[None], agreement), axis=0)
    labels_wide = padded(labels, (("row", 1), ("col", 2)), 3)
    row_ids = lax.axis_index("row") * tile_rows + jnp.arange(-3, tile_rows + 3, dtype=jnp.int32)
    col_ids = lax.axis_index("col") * tile_cols + jnp.arange(-3, tile_cols + 3, dtype=jnp.int32)
    row_in = ((row_ids >= 0) & (row_ids < total_rows)).astype(jnp.float32)
    col_in = ((col_ids >= 0) & (col_ids < total_cols)).astype(jnp.float32)
    inside = row_in[:, None] * col_in[None, :]
    levels = labels_wide[0].astype(jnp.float32)
    counts = labels_wide[1:].astype(jnp.float32)
    weights = neighbour_weights(levels, counts, inside)
    scales = degree_scales(weights)
    row_ends = row_count - 1
    head = basis_block[:, :2, :]
    tail = basis_block[:, tile_rows - 2 :, :]
    from_above = lax.ppermute(tail, "row", [(i, i + 1) for i in range(row_ends)])
    from_below = lax.ppermute(head, "row", [(i + 1, i) for i in range(row_ends)])
    pixels = jnp.concatenate(
        [jnp.transpose(part, (1, 2, 0)) for part in (from_above, basis_block, from_below)], axis=0
    )
    extended = padded(pixels, (("col", 1),), 2)
    first = apply_pixels(extended, pass_coefficients([cropped(w, 1) for w in weights], scales))
    tile_scales = cropped(scales, 1)
    filtered = apply_pixels(first, pass_coefficients([cropped(w, 2) for w in weights], tile_scales))
    pixel_total = float(total_rows * total_cols)
    gram_local = jnp.einsum(
        "rck,rcj->kj", filtered, filtered,
        precision=lax.Precision.HIGH, preferred_element_type=jnp.float32,
    )
    gram = all_sum(all_sum(gram_local, "col"), "row") / pixel_total
    factor = jnp.linalg.cholesky(gram)
    inverse = jax.scipy.linalg.solve_triangular(
        factor, jnp.eye(vectors, dtype=jnp.float32), lower=True
    )
    ortho = jnp.einsum(
        "kj,rcj->krc", inverse, filtered,
        precision=lax.Precision.HIGH, preferred_element_type=jnp.float32,
    )
    return (ortho, factor.T)


def solution(mesh):
    return jax.shard_map(
        per_device,
        mesh=mesh,
        in_specs=(P("row", "col"), P(None, "row", "col"), P(None, "row", "col")),
        out_specs=(P(None, "row", "col"), P()),
        check_vma=False,
    )
```

```python
import jax
import jax.numpy as jnp
from jax import lax
from jax.sharding import PartitionSpec as P

INV_SIGMA = 1.0 / 40.0
NEIGHBOURS = (
    (0, 1, 0, 1, 1.0 / 9.0),
    (0, -1, 0, 0, 1.0 / 9.0),
    (1, 0, 1, 1, 1.0 / 9.0),
    (-1, 0, 1, 0, 1.0 / 9.0),
    (1, 1, 2, 1, 1.0 / 18.0),
    (-1, -1, 2, 0, 1.0 / 18.0),
    (1, -1, 3, 1, 1.0 / 18.0),
    (-1, 1, 3, 0, 1.0 / 18.0),
)


def padded(cells, sides, width):
    for axis, dim in sides:
        count = lax.axis_size(axis)
        ends = count - 1
        head = lax.slice_in_dim(cells, 0, width, axis=dim)
        tail = lax.slice_in_dim(cells, cells.shape[dim] - width, cells.shape[dim], axis=dim)
        cells = jnp.concatenate(
            [
                lax.ppermute(tail, axis, [(i, (i + 1) % count) for i in range(ends)]),
                cells,
                lax.ppermute(head, axis, [((i + 1) % count, i) for i in range(ends)]),
            ],
            axis=dim,
        )
    return cells


def shifted(array, step_row, step_col):
    height = array.shape[-2]
    width = array.shape[-1]
    return array[..., 1 + step_row : height - 1 + step_row, 1 + step_col : width - 1 + step_col]


def cropped(array, cycle):
    return array[..., cycle:-cycle, cycle:-cycle]


def neighbour_weights(levels, counts, inside):
    center = shifted(levels, 0, 0)
    center_in = shifted(inside, 0, 0)
    result = []
    for step_row, step_col, channel, at_center, factor in NEIGHBOURS:
        other = shifted(levels, step_row, step_col)
        if at_center == 1:
            source = shifted(counts[channel], 0, 0)
        else:
            source = shifted(counts[channel], step_row, step_col)
        gap = (center - other) * INV_SIGMA
        result.append(
            (1.0 + source)
            * factor
            * jnp.exp(-gap * gap)
            * center_in
            * shifted(inside, step_row, step_col)
        )
    return result


def degree_scales(weights):
    degree = weights[0]
    for weight in weights[1:]:
        degree = degree + weight
    return lax.rsqrt(1.0 + degree)


def apply_once(values_in, weights, scales):
    lifted = values_in * scales
    summed = None
    for weight, entry in zip(weights, NEIGHBOURS):
        term = weight * shifted(lifted, entry[0], entry[1])
        summed = term if summed is None else summed + term
    return shifted(values_in, 0, 0) - shifted(scales, 0, 0) * summed


def shifted_pixels(array, step_row, step_col):
    height = array.shape[0]
    width = array.shape[1]
    return array[1 + step_row : height - 1 + step_row, 1 + step_col : width - 1 + step_col]


def pass_coefficients(weights, scales):
    center = shifted(scales, 0, 0)
    return jnp.stack(
        [center * weight * shifted(scales, entry[0], entry[1]) for weight, entry in zip(weights, NEIGHBOURS)]
    )


def apply_pixels(values_in, coefficients):
    summed = None
    for index, entry in enumerate(NEIGHBOURS):
        term = coefficients[index][:, :, None] * shifted_pixels(values_in, entry[0], entry[1])
        summed = term if summed is None else summed + term
    return shifted_pixels(values_in, 0, 0) - summed


def exchange_sum(block, axis, low_bit, bits):
    count = lax.axis_size(axis)
    received = [block]
    for offset in range(1, 1 << bits):
        flip = offset << low_bit
        route = [(i, i ^ flip) for i in range(count)]
        received.append(lax.ppermute(block, axis, route))
    while len(received) > 1:
        received = [received[i] + received[i + 1] for i in range(0, len(received), 2)]
    return received[0]


def all_sum(block, axis):
    count = lax.axis_size(axis)
    levels = count.bit_length() - 1
    if (1 << levels) != count:
        return lax.psum(block, axis)
    low_bit = 0
    while low_bit < levels:
        bits = min(2, levels - low_bit)
        block = exchange_sum(block, axis, low_bit, bits)
        low_bit += bits
    return block


def per_device(intensity, agreement, basis_block):
    vectors, tile_rows, tile_cols = basis_block.shape
    row_count = lax.axis_size("row")
    col_count = lax.axis_size("col")
    total_rows = tile_rows * row_count
    total_cols = tile_cols * col_count
    labels = jnp.concatenate((intensity[None], agreement), axis=0)
    labels_wide = padded(labels, (("row", 1), ("col", 2)), 3)
    row_ids = lax.axis_index("row") * tile_rows + jnp.arange(-3, tile_rows + 3, dtype=jnp.int32)
    col_ids = lax.axis_index("col") * tile_cols + jnp.arange(-3, tile_cols + 3, dtype=jnp.int32)
    row_in = ((row_ids >= 0) & (row_ids < total_rows)).astype(jnp.float32)
    col_in = ((col_ids >= 0) & (col_ids < total_cols)).astype(jnp.float32)
    inside = row_in[:, None] * col_in[None, :]
    levels = labels_wide[0].astype(jnp.float32)
    counts = labels_wide[1:].astype(jnp.float32)
    weights = neighbour_weights(levels, counts, inside)
    scales = degree_scales(weights)
    row_ends = row_count - 1
    head = basis_block[:, :2, :]
    tail = basis_block[:, tile_rows - 2 :, :]
    from_above = lax.ppermute(tail, "row", [(i, i + 1) for i in range(row_ends)])
    from_below = lax.ppermute(head, "row", [(i + 1, i) for i in range(row_ends)])
    pixels = jnp.concatenate(
        [jnp.transpose(part, (1, 2, 0)) for part in (from_above, basis_block, from_below)], axis=0
    )
    extended = padded(pixels, (("col", 1),), 2)
    ring_coefficients = pass_coefficients([cropped(w, 1) for w in weights], scales)
    core = apply_pixels(pixels, ring_coefficients[:, :, 2 : tile_cols])
    left = apply_pixels(extended[:, :4], ring_coefficients[:, :, :2])
    right = apply_pixels(extended[:, tile_cols:], ring_coefficients[:, :, tile_cols:])
    first = jnp.concatenate([left, core, right], axis=1)
    tile_scales = cropped(scales, 1)
    filtered = apply_pixels(first, pass_coefficients([cropped(w, 2) for w in weights], tile_scales))
    pixel_total = float(total_rows * total_cols)
    gram_local = jnp.einsum(
        "rck,rcj->kj", filtered, filtered,
        precision=lax.Precision.HIGH, preferred_element_type=jnp.float32,
    )
    gram = all_sum(all_sum(gram_local, "col"), "row") / pixel_total
    factor = jnp.linalg.cholesky(gram)
    inverse = jax.scipy.linalg.solve_triangular(
        factor, jnp.eye(vectors, dtype=jnp.float32), lower=True
    )
    ortho = jnp.einsum(
        "kj,rcj->krc", inverse, filtered,
        precision=lax.Precision.HIGH, preferred_element_type=jnp.float32,
    )
    return (ortho, factor.T)


def solution(mesh):
    return jax.shard_map(
        per_device,
        mesh=mesh,
        in_specs=(P("row", "col"), P(None, "row", "col"), P(None, "row", "col")),
        out_specs=(P(None, "row", "col"), P()),
        check_vma=False,
    )
```

```python
import jax
import jax.numpy as jnp
from jax import lax
from jax.sharding import PartitionSpec as P

INV_SIGMA = 1.0 / 40.0
NEIGHBOURS = (
    (0, 1, 0, 1, 1.0 / 9.0),
    (0, -1, 0, 0, 1.0 / 9.0),
    (1, 0, 1, 1, 1.0 / 9.0),
    (-1, 0, 1, 0, 1.0 / 9.0),
    (1, 1, 2, 1, 1.0 / 18.0),
    (-1, -1, 2, 0, 1.0 / 18.0),
    (1, -1, 3, 1, 1.0 / 18.0),
    (-1, 1, 3, 0, 1.0 / 18.0),
)


def padded(cells, sides, width):
    for axis, dim in sides:
        count = lax.axis_size(axis)
        ends = count - 1
        head = lax.slice_in_dim(cells, 0, width, axis=dim)
        tail = lax.slice_in_dim(cells, cells.shape[dim] - width, cells.shape[dim], axis=dim)
        cells = jnp.concatenate(
            [
                lax.ppermute(tail, axis, [(i, (i + 1) % count) for i in range(ends)]),
                cells,
                lax.ppermute(head, axis, [((i + 1) % count, i) for i in range(ends)]),
            ],
            axis=dim,
        )
    return cells


def shifted(array, step_row, step_col):
    height = array.shape[-2]
    width = array.shape[-1]
    return array[..., 1 + step_row : height - 1 + step_row, 1 + step_col : width - 1 + step_col]


def cropped(array, cycle):
    return array[..., cycle:-cycle, cycle:-cycle]


def neighbour_weights(levels, counts, inside):
    center = shifted(levels, 0, 0)
    center_in = shifted(inside, 0, 0)
    result = []
    for step_row, step_col, channel, at_center, factor in NEIGHBOURS:
        other = shifted(levels, step_row, step_col)
        if at_center == 1:
            source = shifted(counts[channel], 0, 0)
        else:
            source = shifted(counts[channel], step_row, step_col)
        gap = (center - other) * INV_SIGMA
        result.append(
            (1.0 + source)
            * factor
            * jnp.exp(-gap * gap)
            * center_in
            * shifted(inside, step_row, step_col)
        )
    return result


def degree_scales(weights):
    degree = weights[0]
    for weight in weights[1:]:
        degree = degree + weight
    return lax.rsqrt(1.0 + degree)


def apply_once(values_in, weights, scales):
    lifted = values_in * scales
    summed = None
    for weight, entry in zip(weights, NEIGHBOURS):
        term = weight * shifted(lifted, entry[0], entry[1])
        summed = term if summed is None else summed + term
    return shifted(values_in, 0, 0) - shifted(scales, 0, 0) * summed


def shifted_pixels(array, step_row, step_col):
    height = array.shape[0]
    width = array.shape[1]
    return array[1 + step_row : height - 1 + step_row, 1 + step_col : width - 1 + step_col]


def pass_coefficients(weights, scales):
    center = shifted(scales, 0, 0)
    return jnp.stack(
        [center * weight * shifted(scales, entry[0], entry[1]) for weight, entry in zip(weights, NEIGHBOURS)]
    )


def apply_pixels(values_in, coefficients):
    summed = None
    for index, entry in enumerate(NEIGHBOURS):
        term = coefficients[index][:, :, None] * shifted_pixels(values_in, entry[0], entry[1])
        summed = term if summed is None else summed + term
    return shifted_pixels(values_in, 0, 0) - summed


def exchange_sum(block, axis, low_bit, bits):
    count = lax.axis_size(axis)
    received = [block]
    for offset in range(1, 1 << bits):
        flip = offset << low_bit
        route = [(i, i ^ flip) for i in range(count)]
        received.append(lax.ppermute(block, axis, route))
    while len(received) > 1:
        received = [received[i] + received[i + 1] for i in range(0, len(received), 2)]
    return received[0]


def all_sum(block, axis):
    count = lax.axis_size(axis)
    levels = count.bit_length() - 1
    if (1 << levels) != count:
        return lax.psum(block, axis)
    low_bit = 0
    while low_bit < levels:
        bits = min(2, levels - low_bit)
        block = exchange_sum(block, axis, low_bit, bits)
        low_bit += bits
    return block


def pack(cells, marks):
    lanes = cells.shape[-1]
    flat = marks.reshape(-1)
    rows = -(-flat.shape[0] // lanes)
    flat = jnp.pad(flat, (0, rows * lanes - flat.shape[0])).reshape(rows, lanes)
    return jnp.concatenate([cells.reshape(-1, lanes), flat], axis=0)


def unpack(block, cells_shape, marks_shape):
    count = cells_shape[0] * cells_shape[1]
    cells = block[:count].reshape(cells_shape)
    size = marks_shape[0] * marks_shape[1] * marks_shape[2]
    marks = block[count:].reshape(-1)[:size].reshape(marks_shape)
    return cells, marks


def per_device(intensity, agreement, basis_block):
    vectors, tile_rows, tile_cols = basis_block.shape
    row_count = lax.axis_size("row")
    col_count = lax.axis_size("col")
    total_rows = tile_rows * row_count
    total_cols = tile_cols * col_count
    row_ends = row_count - 1
    col_ends = col_count - 1
    down = [(i, i + 1) for i in range(row_ends)]
    up = [(i + 1, i) for i in range(row_ends)]
    rightward = [(i, i + 1) for i in range(col_ends)]
    leftward = [(i + 1, i) for i in range(col_ends)]
    labels = jnp.concatenate((intensity[None], agreement), axis=0).astype(jnp.float32)
    head = jnp.concatenate([basis_block[:, :3, :], labels[:, :3, :]], axis=0)
    tail = jnp.concatenate([basis_block[:, tile_rows - 3 :, :], labels[:, tile_rows - 3 :, :]], axis=0)
    from_above = lax.ppermute(tail, "row", down)
    from_below = lax.ppermute(head, "row", up)
    label_rows = jnp.concatenate([from_above[vectors:], labels, from_below[vectors:]], axis=1)
    pixels = jnp.concatenate(
        [
            jnp.transpose(part, (1, 2, 0))
            for part in (from_above[:vectors, 1:], basis_block, from_below[:vectors, :2])
        ],
        axis=0,
    )
    west = pack(pixels[:, :2, :], label_rows[:, :, :3])
    east = pack(pixels[:, tile_cols - 2 :, :], label_rows[:, :, tile_cols - 3 :])
    from_left = lax.ppermute(east, "col", rightward)
    from_right = lax.ppermute(west, "col", leftward)
    left_cells, left_labels = unpack(from_left, (pixels.shape[0], 2, vectors), (labels.shape[0], label_rows.shape[1], 3))
    right_cells, right_labels = unpack(from_right, (pixels.shape[0], 2, vectors), (labels.shape[0], label_rows.shape[1], 3))
    extended = jnp.concatenate([left_cells, pixels, right_cells], axis=1)
    labels_wide = jnp.concatenate([left_labels, label_rows, right_labels], axis=2)
    row_ids = lax.axis_index("row") * tile_rows + jnp.arange(-3, tile_rows + 3, dtype=jnp.int32)
    col_ids = lax.axis_index("col") * tile_cols + jnp.arange(-3, tile_cols + 3, dtype=jnp.int32)
    row_in = ((row_ids >= 0) & (row_ids < total_rows)).astype(jnp.float32)
    col_in = ((col_ids >= 0) & (col_ids < total_cols)).astype(jnp.float32)
    inside = row_in[:, None] * col_in[None, :]
    levels = labels_wide[0]
    counts = labels_wide[1:]
    weights = neighbour_weights(levels, counts, inside)
    scales = degree_scales(weights)
    first = apply_pixels(extended, pass_coefficients([cropped(w, 1) for w in weights], scales))
    tile_scales = cropped(scales, 1)
    filtered = apply_pixels(first, pass_coefficients([cropped(w, 2) for w in weights], tile_scales))
    pixel_total = float(total_rows * total_cols)
    gram_local = jnp.einsum(
        "rck,rcj->kj", filtered, filtered,
        precision=lax.Precision.HIGH, preferred_element_type=jnp.float32,
    )
    gram = all_sum(all_sum(gram_local, "col"), "row") / pixel_total
    factor = jnp.linalg.cholesky(gram)
    inverse = jax.scipy.linalg.solve_triangular(
        factor, jnp.eye(vectors, dtype=jnp.float32), lower=True
    )
    ortho = jnp.einsum(
        "kj,rcj->krc", inverse, filtered,
        precision=lax.Precision.HIGH, preferred_element_type=jnp.float32,
    )
    return (ortho, factor.T)


def solution(mesh):
    return jax.shard_map(
        per_device,
        mesh=mesh,
        in_specs=(P("row", "col"), P(None, "row", "col"), P(None, "row", "col")),
        out_specs=(P(None, "row", "col"), P()),
        check_vma=False,
    )
```

```python
import jax
import jax.numpy as jnp
from jax import lax
from jax.sharding import PartitionSpec as P

INV_SIGMA = 1.0 / 40.0
NEIGHBOURS = (
    (0, 1, 0, 1, 1.0 / 9.0),
    (0, -1, 0, 0, 1.0 / 9.0),
    (1, 0, 1, 1, 1.0 / 9.0),
    (-1, 0, 1, 0, 1.0 / 9.0),
    (1, 1, 2, 1, 1.0 / 18.0),
    (-1, -1, 2, 0, 1.0 / 18.0),
    (1, -1, 3, 1, 1.0 / 18.0),
    (-1, 1, 3, 0, 1.0 / 18.0),
)


def padded(cells, sides, width):
    for axis, dim in sides:
        count = lax.axis_size(axis)
        ends = count - 1
        head = lax.slice_in_dim(cells, 0, width, axis=dim)
        tail = lax.slice_in_dim(cells, cells.shape[dim] - width, cells.shape[dim], axis=dim)
        cells = jnp.concatenate(
            [
                lax.ppermute(tail, axis, [(i, (i + 1) % count) for i in range(ends)]),
                cells,
                lax.ppermute(head, axis, [((i + 1) % count, i) for i in range(ends)]),
            ],
            axis=dim,
        )
    return cells


def shifted(array, step_row, step_col):
    height = array.shape[-2]
    width = array.shape[-1]
    return array[..., 1 + step_row : height - 1 + step_row, 1 + step_col : width - 1 + step_col]


def cropped(array, cycle):
    return array[..., cycle:-cycle, cycle:-cycle]


def neighbour_weights(levels, counts, inside):
    center = shifted(levels, 0, 0)
    center_in = shifted(inside, 0, 0)
    result = []
    for step_row, step_col, channel, at_center, factor in NEIGHBOURS:
        other = shifted(levels, step_row, step_col)
        if at_center == 1:
            source = shifted(counts[channel], 0, 0)
        else:
            source = shifted(counts[channel], step_row, step_col)
        gap = (center - other) * INV_SIGMA
        result.append(
            (1.0 + source)
            * factor
            * jnp.exp(-gap * gap)
            * center_in
            * shifted(inside, step_row, step_col)
        )
    return result


def degree_scales(weights):
    degree = weights[0]
    for weight in weights[1:]:
        degree = degree + weight
    return lax.rsqrt(1.0 + degree)


def apply_once(values_in, weights, scales):
    lifted = values_in * scales
    summed = None
    for weight, entry in zip(weights, NEIGHBOURS):
        term = weight * shifted(lifted, entry[0], entry[1])
        summed = term if summed is None else summed + term
    return shifted(values_in, 0, 0) - shifted(scales, 0, 0) * summed


def shifted_pixels(array, step_row, step_col):
    height = array.shape[0]
    width = array.shape[1]
    return array[1 + step_row : height - 1 + step_row, 1 + step_col : width - 1 + step_col]


def pass_coefficients(weights, scales):
    center = shifted(scales, 0, 0)
    return jnp.stack(
        [center * weight * shifted(scales, entry[0], entry[1]) for weight, entry in zip(weights, NEIGHBOURS)]
    )


def apply_pixels(values_in, coefficients):
    summed = None
    for index, entry in enumerate(NEIGHBOURS):
        term = coefficients[index][:, :, None] * shifted_pixels(values_in, entry[0], entry[1])
        summed = term if summed is None else summed + term
    return shifted_pixels(values_in, 0, 0) - summed


def exchange_sum(block, axis, low_bit, bits):
    count = lax.axis_size(axis)
    received = [block]
    for offset in range(1, 1 << bits):
        flip = offset << low_bit
        route = [(i, i ^ flip) for i in range(count)]
        received.append(lax.ppermute(block, axis, route))
    while len(received) > 1:
        received = [received[i] + received[i + 1] for i in range(0, len(received), 2)]
    return received[0]


def all_sum(block, axis):
    count = lax.axis_size(axis)
    levels = count.bit_length() - 1
    if (1 << levels) != count:
        return lax.psum(block, axis)
    low_bit = 0
    while low_bit < levels:
        bits = min(2, levels - low_bit)
        block = exchange_sum(block, axis, low_bit, bits)
        low_bit += bits
    return block


def pack(cells, marks):
    rows, width, lanes = cells.shape
    flat = marks.reshape(-1)
    flat = jnp.pad(flat, (0, rows * lanes - flat.shape[0])).reshape(rows, 1, lanes)
    return jnp.concatenate([cells, flat], axis=1)


def unpack(block, marks_shape):
    width = block.shape[1] - 1
    size = marks_shape[0] * marks_shape[1] * marks_shape[2]
    marks = block[:, width:].reshape(-1)[:size].reshape(marks_shape)
    return block[:, :width], marks


def per_device(intensity, agreement, basis_block):
    vectors, tile_rows, tile_cols = basis_block.shape
    row_count = lax.axis_size("row")
    col_count = lax.axis_size("col")
    total_rows = tile_rows * row_count
    total_cols = tile_cols * col_count
    row_ends = row_count - 1
    col_ends = col_count - 1
    down = [(i, i + 1) for i in range(row_ends)]
    up = [(i + 1, i) for i in range(row_ends)]
    rightward = [(i, i + 1) for i in range(col_ends)]
    leftward = [(i + 1, i) for i in range(col_ends)]
    labels = jnp.concatenate((intensity[None], agreement), axis=0).astype(jnp.float32)
    head = jnp.concatenate([basis_block[:, :3, :], labels[:, :3, :]], axis=0)
    tail = jnp.concatenate([basis_block[:, tile_rows - 3 :, :], labels[:, tile_rows - 3 :, :]], axis=0)
    from_above = lax.ppermute(tail, "row", down)
    from_below = lax.ppermute(head, "row", up)
    label_rows = jnp.concatenate([from_above[vectors:], labels, from_below[vectors:]], axis=1)
    pixels = jnp.concatenate(
        [
            jnp.transpose(part, (1, 2, 0))
            for part in (from_above[:vectors, 1:], basis_block, from_below[:vectors, :2])
        ],
        axis=0,
    )
    west = pack(pixels[:, :2, :], label_rows[:, :, :3])
    east = pack(pixels[:, tile_cols - 2 :, :], label_rows[:, :, tile_cols - 3 :])
    from_left = lax.ppermute(east, "col", rightward)
    from_right = lax.ppermute(west, "col", leftward)
    left_cells, left_labels = unpack(from_left, (labels.shape[0], label_rows.shape[1], 3))
    right_cells, right_labels = unpack(from_right, (labels.shape[0], label_rows.shape[1], 3))
    extended = jnp.concatenate([left_cells, pixels, right_cells], axis=1)
    labels_wide = jnp.concatenate([left_labels, label_rows, right_labels], axis=2)
    row_ids = lax.axis_index("row") * tile_rows + jnp.arange(-3, tile_rows + 3, dtype=jnp.int32)
    col_ids = lax.axis_index("col") * tile_cols + jnp.arange(-3, tile_cols + 3, dtype=jnp.int32)
    row_in = ((row_ids >= 0) & (row_ids < total_rows)).astype(jnp.float32)
    col_in = ((col_ids >= 0) & (col_ids < total_cols)).astype(jnp.float32)
    inside = row_in[:, None] * col_in[None, :]
    levels = labels_wide[0]
    counts = labels_wide[1:]
    weights = neighbour_weights(levels, counts, inside)
    scales = degree_scales(weights)
    first = apply_pixels(extended, pass_coefficients([cropped(w, 1) for w in weights], scales))
    tile_scales = cropped(scales, 1)
    filtered = apply_pixels(first, pass_coefficients([cropped(w, 2) for w in weights], tile_scales))
    pixel_total = float(total_rows * total_cols)
    gram_local = jnp.einsum(
        "rck,rcj->kj", filtered, filtered,
        precision=lax.Precision.HIGH, preferred_element_type=jnp.float32,
    )
    gram = all_sum(all_sum(gram_local, "col"), "row") / pixel_total
    factor = jnp.linalg.cholesky(gram)
    inverse = jax.scipy.linalg.solve_triangular(
        factor, jnp.eye(vectors, dtype=jnp.float32), lower=True
    )
    ortho = jnp.einsum(
        "kj,rcj->krc", inverse, filtered,
        precision=lax.Precision.HIGH, preferred_element_type=jnp.float32,
    )
    return (ortho, factor.T)


def solution(mesh):
    return jax.shard_map(
        per_device,
        mesh=mesh,
        in_specs=(P("row", "col"), P(None, "row", "col"), P(None, "row", "col")),
        out_specs=(P(None, "row", "col"), P()),
        check_vma=False,
    )
```

```python
import jax
import jax.numpy as jnp
from jax import lax
from jax.sharding import PartitionSpec as P

INV_SIGMA = 1.0 / 40.0
NEIGHBOURS = (
    (0, 1, 0, 1, 1.0 / 9.0),
    (0, -1, 0, 0, 1.0 / 9.0),
    (1, 0, 1, 1, 1.0 / 9.0),
    (-1, 0, 1, 0, 1.0 / 9.0),
    (1, 1, 2, 1, 1.0 / 18.0),
    (-1, -1, 2, 0, 1.0 / 18.0),
    (1, -1, 3, 1, 1.0 / 18.0),
    (-1, 1, 3, 0, 1.0 / 18.0),
)


def padded(cells, sides, width):
    for axis, dim in sides:
        count = lax.axis_size(axis)
        ends = count - 1
        head = lax.slice_in_dim(cells, 0, width, axis=dim)
        tail = lax.slice_in_dim(cells, cells.shape[dim] - width, cells.shape[dim], axis=dim)
        cells = jnp.concatenate(
            [
                lax.ppermute(tail, axis, [(i, (i + 1) % count) for i in range(ends)]),
                cells,
                lax.ppermute(head, axis, [((i + 1) % count, i) for i in range(ends)]),
            ],
            axis=dim,
        )
    return cells


def shifted(array, step_row, step_col):
    height = array.shape[-2]
    width = array.shape[-1]
    return array[..., 1 + step_row : height - 1 + step_row, 1 + step_col : width - 1 + step_col]


def cropped(array, cycle):
    return array[..., cycle:-cycle, cycle:-cycle]


def neighbour_weights(levels, counts, inside):
    center = shifted(levels, 0, 0)
    center_in = shifted(inside, 0, 0)
    result = []
    for step_row, step_col, channel, at_center, factor in NEIGHBOURS:
        other = shifted(levels, step_row, step_col)
        if at_center == 1:
            source = shifted(counts[channel], 0, 0)
        else:
            source = shifted(counts[channel], step_row, step_col)
        gap = (center - other) * INV_SIGMA
        result.append(
            (1.0 + source)
            * factor
            * jnp.exp(-gap * gap)
            * center_in
            * shifted(inside, step_row, step_col)
        )
    return result


def degree_scales(weights):
    degree = weights[0]
    for weight in weights[1:]:
        degree = degree + weight
    return lax.rsqrt(1.0 + degree)


def apply_once(values_in, weights, scales):
    lifted = values_in * scales
    summed = None
    for weight, entry in zip(weights, NEIGHBOURS):
        term = weight * shifted(lifted, entry[0], entry[1])
        summed = term if summed is None else summed + term
    return shifted(values_in, 0, 0) - shifted(scales, 0, 0) * summed


def shifted_pixels(array, step_row, step_col):
    height = array.shape[0]
    width = array.shape[1]
    return array[1 + step_row : height - 1 + step_row, 1 + step_col : width - 1 + step_col]


def pass_coefficients(weights, scales):
    center = shifted(scales, 0, 0)
    return jnp.stack(
        [center * weight * shifted(scales, entry[0], entry[1]) for weight, entry in zip(weights, NEIGHBOURS)]
    )


def apply_pixels(values_in, coefficients):
    summed = None
    for index, entry in enumerate(NEIGHBOURS):
        term = coefficients[index][:, :, None] * shifted_pixels(values_in, entry[0], entry[1])
        summed = term if summed is None else summed + term
    return shifted_pixels(values_in, 0, 0) - summed


def exchange_sum(block, axis, low_bit, bits):
    count = lax.axis_size(axis)
    received = [block]
    for offset in range(1, 1 << bits):
        flip = offset << low_bit
        route = [(i, i ^ flip) for i in range(count)]
        received.append(lax.ppermute(block, axis, route))
    while len(received) > 1:
        received = [received[i] + received[i + 1] for i in range(0, len(received), 2)]
    return received[0]


def all_sum(block, axis):
    count = lax.axis_size(axis)
    levels = count.bit_length() - 1
    if (1 << levels) != count:
        return lax.psum(block, axis)
    low_bit = 0
    while low_bit < levels:
        bits = min(2, levels - low_bit)
        block = exchange_sum(block, axis, low_bit, bits)
        low_bit += bits
    return block


def per_device(intensity, agreement, basis_block):
    vectors, tile_rows, tile_cols = basis_block.shape
    row_count = lax.axis_size("row")
    col_count = lax.axis_size("col")
    total_rows = tile_rows * row_count
    total_cols = tile_cols * col_count
    labels = jnp.concatenate((intensity[None], agreement), axis=0)
    labels_wide = padded(labels, (("row", 1), ("col", 2)), 3)
    row_ids = lax.axis_index("row") * tile_rows + jnp.arange(-3, tile_rows + 3, dtype=jnp.int32)
    col_ids = lax.axis_index("col") * tile_cols + jnp.arange(-3, tile_cols + 3, dtype=jnp.int32)
    row_in = ((row_ids >= 0) & (row_ids < total_rows)).astype(jnp.float32)
    col_in = ((col_ids >= 0) & (col_ids < total_cols)).astype(jnp.float32)
    inside = row_in[:, None] * col_in[None, :]
    levels = labels_wide[0].astype(jnp.float32)
    counts = labels_wide[1:].astype(jnp.float32)
    weights = neighbour_weights(levels, counts, inside)
    scales = degree_scales(weights)
    pixels = jnp.transpose(basis_block, (1, 2, 0))
    extended = padded(pixels, (("row", 0), ("col", 1)), 2)
    first = apply_pixels(extended, pass_coefficients([cropped(w, 1) for w in weights], scales))
    tile_scales = cropped(scales, 1)
    filtered = apply_pixels(first, pass_coefficients([cropped(w, 2) for w in weights], tile_scales))
    pixel_total = float(total_rows * total_cols)
    gram_local = jnp.einsum(
        "rck,rcj->kj", filtered, filtered,
        precision=lax.Precision.HIGHEST, preferred_element_type=jnp.float32,
    )
    gram = all_sum(all_sum(gram_local, "col"), "row") / pixel_total
    factor = jnp.linalg.cholesky(gram)
    inverse = jax.scipy.linalg.solve_triangular(
        factor, jnp.eye(vectors, dtype=jnp.float32), lower=True
    )
    ortho = jnp.einsum(
        "kj,rcj->krc", inverse, filtered,
        precision=lax.Precision.HIGHEST, preferred_element_type=jnp.float32,
    )
    return (ortho, factor.T)


def solution(mesh):
    return jax.shard_map(
        per_device,
        mesh=mesh,
        in_specs=(P("row", "col"), P(None, "row", "col"), P(None, "row", "col")),
        out_specs=(P(None, "row", "col"), P()),
        check_vma=False,
    )
```

```python
import jax
import jax.numpy as jnp
from jax import lax
from jax.sharding import PartitionSpec as P

INV_SIGMA = 1.0 / 40.0
NEIGHBOURS = (
    (0, 1, 0, 1, 1.0 / 9.0),
    (0, -1, 0, 0, 1.0 / 9.0),
    (1, 0, 1, 1, 1.0 / 9.0),
    (-1, 0, 1, 0, 1.0 / 9.0),
    (1, 1, 2, 1, 1.0 / 18.0),
    (-1, -1, 2, 0, 1.0 / 18.0),
    (1, -1, 3, 1, 1.0 / 18.0),
    (-1, 1, 3, 0, 1.0 / 18.0),
)


def padded(cells, sides, width):
    for axis, dim in sides:
        count = lax.axis_size(axis)
        ends = count - 1
        head = lax.slice_in_dim(cells, 0, width, axis=dim)
        tail = lax.slice_in_dim(cells, cells.shape[dim] - width, cells.shape[dim], axis=dim)
        cells = jnp.concatenate(
            [
                lax.ppermute(tail, axis, [(i, (i + 1) % count) for i in range(ends)]),
                cells,
                lax.ppermute(head, axis, [((i + 1) % count, i) for i in range(ends)]),
            ],
            axis=dim,
        )
    return cells


def shifted(array, step_row, step_col):
    height = array.shape[-2]
    width = array.shape[-1]
    return array[..., 1 + step_row : height - 1 + step_row, 1 + step_col : width - 1 + step_col]


def cropped(array, cycle):
    return array[..., cycle:-cycle, cycle:-cycle]


def neighbour_weights(levels, counts, inside):
    center = shifted(levels, 0, 0)
    center_in = shifted(inside, 0, 0)
    result = []
    for step_row, step_col, channel, at_center, factor in NEIGHBOURS:
        other = shifted(levels, step_row, step_col)
        if at_center == 1:
            source = shifted(counts[channel], 0, 0)
        else:
            source = shifted(counts[channel], step_row, step_col)
        gap = (center - other) * INV_SIGMA
        result.append(
            (1.0 + source)
            * factor
            * jnp.exp(-gap * gap)
            * center_in
            * shifted(inside, step_row, step_col)
        )
    return result


def degree_scales(weights):
    degree = weights[0]
    for weight in weights[1:]:
        degree = degree + weight
    return lax.rsqrt(1.0 + degree)


def apply_once(values_in, weights, scales):
    lifted = values_in * scales
    summed = None
    for weight, entry in zip(weights, NEIGHBOURS):
        term = weight * shifted(lifted, entry[0], entry[1])
        summed = term if summed is None else summed + term
    return shifted(values_in, 0, 0) - shifted(scales, 0, 0) * summed


def shifted_pixels(array, step_row, step_col):
    height = array.shape[0]
    width = array.shape[1]
    return array[1 + step_row : height - 1 + step_row, 1 + step_col : width - 1 + step_col]


def pass_coefficients(weights, scales):
    center = shifted(scales, 0, 0)
    return jnp.stack(
        [center * weight * shifted(scales, entry[0], entry[1]) for weight, entry in zip(weights, NEIGHBOURS)]
    )


def apply_pixels(values_in, coefficients):
    summed = None
    for index, entry in enumerate(NEIGHBOURS):
        term = coefficients[index][:, :, None] * shifted_pixels(values_in, entry[0], entry[1])
        summed = term if summed is None else summed + term
    return shifted_pixels(values_in, 0, 0) - summed


def exchange_sum(block, axis, low_bit, bits):
    count = lax.axis_size(axis)
    received = [block]
    for offset in range(1, 1 << bits):
        flip = offset << low_bit
        route = [(i, i ^ flip) for i in range(count)]
        received.append(lax.ppermute(block, axis, route))
    while len(received) > 1:
        received = [received[i] + received[i + 1] for i in range(0, len(received), 2)]
    return received[0]


def all_sum(block, axis):
    count = lax.axis_size(axis)
    levels = count.bit_length() - 1
    if (1 << levels) != count:
        return lax.psum(block, axis)
    low_bit = 0
    while low_bit < levels:
        bits = min(2, levels - low_bit)
        block = exchange_sum(block, axis, low_bit, bits)
        low_bit += bits
    return block


def per_device(intensity, agreement, basis_block):
    vectors, tile_rows, tile_cols = basis_block.shape
    row_count = lax.axis_size("row")
    col_count = lax.axis_size("col")
    total_rows = tile_rows * row_count
    total_cols = tile_cols * col_count
    labels = jnp.concatenate((intensity[None], agreement), axis=0)
    labels_wide = padded(labels, (("row", 1), ("col", 2)), 3)
    row_ids = lax.axis_index("row") * tile_rows + jnp.arange(-3, tile_rows + 3, dtype=jnp.int32)
    col_ids = lax.axis_index("col") * tile_cols + jnp.arange(-3, tile_cols + 3, dtype=jnp.int32)
    row_in = ((row_ids >= 0) & (row_ids < total_rows)).astype(jnp.float32)
    col_in = ((col_ids >= 0) & (col_ids < total_cols)).astype(jnp.float32)
    inside = row_in[:, None] * col_in[None, :]
    levels = labels_wide[0].astype(jnp.float32)
    counts = labels_wide[1:].astype(jnp.float32)
    weights = neighbour_weights(levels, counts, inside)
    scales = degree_scales(weights)
    pixels = jnp.transpose(basis_block, (1, 2, 0))
    extended = padded(pixels, (("row", 0), ("col", 1)), 2)
    first = apply_pixels(extended, pass_coefficients([cropped(w, 1) for w in weights], scales))
    tile_scales = cropped(scales, 1)
    filtered = apply_pixels(first, pass_coefficients([cropped(w, 2) for w in weights], tile_scales))
    pixel_total = float(total_rows * total_cols)
    gram_local = jnp.einsum(
        "rck,rcj->kj", filtered, filtered,
        precision=lax.Precision.HIGHEST, preferred_element_type=jnp.float32,
    )
    gram = all_sum(all_sum(gram_local, "row"), "col") / pixel_total
    factor = jnp.linalg.cholesky(gram)
    inverse = jax.scipy.linalg.solve_triangular(
        factor, jnp.eye(vectors, dtype=jnp.float32), lower=True
    )
    ortho = jnp.einsum(
        "kj,rcj->krc", inverse, filtered,
        precision=lax.Precision.HIGHEST, preferred_element_type=jnp.float32,
    )
    return (ortho, factor.T)


def solution(mesh):
    return jax.shard_map(
        per_device,
        mesh=mesh,
        in_specs=(P("row", "col"), P(None, "row", "col"), P(None, "row", "col")),
        out_specs=(P(None, "row", "col"), P()),
        check_vma=False,
    )
```

```python
import jax
import jax.numpy as jnp
from jax import lax
from jax.sharding import PartitionSpec as P

INV_SIGMA = 1.0 / 40.0
NEIGHBOURS = (
    (0, 1, 0, 1, 1.0 / 9.0),
    (0, -1, 0, 0, 1.0 / 9.0),
    (1, 0, 1, 1, 1.0 / 9.0),
    (-1, 0, 1, 0, 1.0 / 9.0),
    (1, 1, 2, 1, 1.0 / 18.0),
    (-1, -1, 2, 0, 1.0 / 18.0),
    (1, -1, 3, 1, 1.0 / 18.0),
    (-1, 1, 3, 0, 1.0 / 18.0),
)


def padded(cells, sides, width):
    for axis, dim in sides:
        count = lax.axis_size(axis)
        ends = count - 1
        head = lax.slice_in_dim(cells, 0, width, axis=dim)
        tail = lax.slice_in_dim(cells, cells.shape[dim] - width, cells.shape[dim], axis=dim)
        cells = jnp.concatenate(
            [
                lax.ppermute(tail, axis, [(i, (i + 1) % count) for i in range(ends)]),
                cells,
                lax.ppermute(head, axis, [((i + 1) % count, i) for i in range(ends)]),
            ],
            axis=dim,
        )
    return cells


def shifted(array, step_row, step_col):
    height = array.shape[-2]
    width = array.shape[-1]
    return array[..., 1 + step_row : height - 1 + step_row, 1 + step_col : width - 1 + step_col]


def cropped(array, cycle):
    return array[..., cycle:-cycle, cycle:-cycle]


def neighbour_weights(levels, counts, inside):
    center = shifted(levels, 0, 0)
    center_in = shifted(inside, 0, 0)
    result = []
    for step_row, step_col, channel, at_center, factor in NEIGHBOURS:
        other = shifted(levels, step_row, step_col)
        if at_center == 1:
            source = shifted(counts[channel], 0, 0)
        else:
            source = shifted(counts[channel], step_row, step_col)
        gap = (center - other) * INV_SIGMA
        result.append(
            (1.0 + source)
            * factor
            * jnp.exp(-gap * gap)
            * center_in
            * shifted(inside, step_row, step_col)
        )
    return result


def degree_scales(weights):
    degree = weights[0]
    for weight in weights[1:]:
        degree = degree + weight
    return lax.rsqrt(1.0 + degree)


def apply_once(values_in, weights, scales):
    lifted = values_in * scales
    summed = None
    for weight, entry in zip(weights, NEIGHBOURS):
        term = weight * shifted(lifted, entry[0], entry[1])
        summed = term if summed is None else summed + term
    return shifted(values_in, 0, 0) - shifted(scales, 0, 0) * summed


def shifted_pixels(array, step_row, step_col):
    height = array.shape[0]
    width = array.shape[1]
    return array[1 + step_row : height - 1 + step_row, 1 + step_col : width - 1 + step_col]


def pass_coefficients(weights, scales):
    center = shifted(scales, 0, 0)
    return jnp.stack(
        [center * weight * shifted(scales, entry[0], entry[1]) for weight, entry in zip(weights, NEIGHBOURS)]
    )


def apply_pixels(values_in, coefficients):
    summed = None
    for index, entry in enumerate(NEIGHBOURS):
        term = coefficients[index][:, :, None] * shifted_pixels(values_in, entry[0], entry[1])
        summed = term if summed is None else summed + term
    return shifted_pixels(values_in, 0, 0) - summed


def exchange_sum(block, axis, low_bit, bits):
    count = lax.axis_size(axis)
    received = [block]
    for offset in range(1, 1 << bits):
        flip = offset << low_bit
        route = [(i, i ^ flip) for i in range(count)]
        received.append(lax.ppermute(block, axis, route))
    while len(received) > 1:
        received = [received[i] + received[i + 1] for i in range(0, len(received), 2)]
    return received[0]


def all_sum(block, axis):
    count = lax.axis_size(axis)
    levels = count.bit_length() - 1
    if (1 << levels) != count:
        return lax.psum(block, axis)
    groups = []
    low_bit = 0
    while low_bit < levels:
        bits = min(2, levels - low_bit)
        groups.append((low_bit, bits))
        low_bit += bits
    for low_bit, bits in reversed(groups):
        block = exchange_sum(block, axis, low_bit, bits)
    return block


def per_device(intensity, agreement, basis_block):
    vectors, tile_rows, tile_cols = basis_block.shape
    row_count = lax.axis_size("row")
    col_count = lax.axis_size("col")
    total_rows = tile_rows * row_count
    total_cols = tile_cols * col_count
    labels = jnp.concatenate((intensity[None], agreement), axis=0)
    labels_wide = padded(labels, (("row", 1), ("col", 2)), 3)
    row_ids = lax.axis_index("row") * tile_rows + jnp.arange(-3, tile_rows + 3, dtype=jnp.int32)
    col_ids = lax.axis_index("col") * tile_cols + jnp.arange(-3, tile_cols + 3, dtype=jnp.int32)
    row_in = ((row_ids >= 0) & (row_ids < total_rows)).astype(jnp.float32)
    col_in = ((col_ids >= 0) & (col_ids < total_cols)).astype(jnp.float32)
    inside = row_in[:, None] * col_in[None, :]
    levels = labels_wide[0].astype(jnp.float32)
    counts = labels_wide[1:].astype(jnp.float32)
    weights = neighbour_weights(levels, counts, inside)
    scales = degree_scales(weights)
    pixels = jnp.transpose(basis_block, (1, 2, 0))
    extended = padded(pixels, (("row", 0), ("col", 1)), 2)
    first = apply_pixels(extended, pass_coefficients([cropped(w, 1) for w in weights], scales))
    tile_scales = cropped(scales, 1)
    filtered = apply_pixels(first, pass_coefficients([cropped(w, 2) for w in weights], tile_scales))
    pixel_total = float(total_rows * total_cols)
    gram_local = jnp.einsum(
        "rck,rcj->kj", filtered, filtered,
        precision=lax.Precision.HIGHEST, preferred_element_type=jnp.float32,
    )
    gram = all_sum(all_sum(gram_local, "row"), "col") / pixel_total
    factor = jnp.linalg.cholesky(gram)
    inverse = jax.scipy.linalg.solve_triangular(
        factor, jnp.eye(vectors, dtype=jnp.float32), lower=True
    )
    ortho = jnp.einsum(
        "kj,rcj->krc", inverse, filtered,
        precision=lax.Precision.HIGHEST, preferred_element_type=jnp.float32,
    )
    return (ortho, factor.T)


def solution(mesh):
    return jax.shard_map(
        per_device,
        mesh=mesh,
        in_specs=(P("row", "col"), P(None, "row", "col"), P(None, "row", "col")),
        out_specs=(P(None, "row", "col"), P()),
        check_vma=False,
    )
```

```python
import jax
import jax.numpy as jnp
from jax import lax
from jax.sharding import PartitionSpec as P

INV_SIGMA = 1.0 / 40.0
NEIGHBOURS = (
    (0, 1, 0, 1, 1.0 / 9.0),
    (0, -1, 0, 0, 1.0 / 9.0),
    (1, 0, 1, 1, 1.0 / 9.0),
    (-1, 0, 1, 0, 1.0 / 9.0),
    (1, 1, 2, 1, 1.0 / 18.0),
    (-1, -1, 2, 0, 1.0 / 18.0),
    (1, -1, 3, 1, 1.0 / 18.0),
    (-1, 1, 3, 0, 1.0 / 18.0),
)


def padded(cells, sides, width):
    for axis, dim in sides:
        count = lax.axis_size(axis)
        ends = count - 1
        head = lax.slice_in_dim(cells, 0, width, axis=dim)
        tail = lax.slice_in_dim(cells, cells.shape[dim] - width, cells.shape[dim], axis=dim)
        cells = jnp.concatenate(
            [
                lax.ppermute(tail, axis, [(i, (i + 1) % count) for i in range(ends)]),
                cells,
                lax.ppermute(head, axis, [((i + 1) % count, i) for i in range(ends)]),
            ],
            axis=dim,
        )
    return cells


def shifted(array, step_row, step_col):
    height = array.shape[-2]
    width = array.shape[-1]
    return array[..., 1 + step_row : height - 1 + step_row, 1 + step_col : width - 1 + step_col]


def cropped(array, cycle):
    return array[..., cycle:-cycle, cycle:-cycle]


def neighbour_weights(levels, counts, inside):
    center = shifted(levels, 0, 0)
    center_in = shifted(inside, 0, 0)
    result = []
    for step_row, step_col, channel, at_center, factor in NEIGHBOURS:
        other = shifted(levels, step_row, step_col)
        if at_center == 1:
            source = shifted(counts[channel], 0, 0)
        else:
            source = shifted(counts[channel], step_row, step_col)
        gap = (center - other) * INV_SIGMA
        result.append(
            (1.0 + source)
            * factor
            * jnp.exp(-gap * gap)
            * center_in
            * shifted(inside, step_row, step_col)
        )
    return result


def degree_scales(weights):
    degree = weights[0]
    for weight in weights[1:]:
        degree = degree + weight
    return lax.rsqrt(1.0 + degree)


def apply_once(values_in, weights, scales):
    lifted = values_in * scales
    summed = None
    for weight, entry in zip(weights, NEIGHBOURS):
        term = weight * shifted(lifted, entry[0], entry[1])
        summed = term if summed is None else summed + term
    return shifted(values_in, 0, 0) - shifted(scales, 0, 0) * summed


def shifted_pixels(array, step_row, step_col):
    height = array.shape[0]
    width = array.shape[1]
    return array[1 + step_row : height - 1 + step_row, 1 + step_col : width - 1 + step_col]


def pass_coefficients(weights, scales):
    center = shifted(scales, 0, 0)
    return jnp.stack(
        [center * weight * shifted(scales, entry[0], entry[1]) for weight, entry in zip(weights, NEIGHBOURS)]
    )


def apply_pixels(values_in, coefficients):
    summed = None
    for index, entry in enumerate(NEIGHBOURS):
        term = coefficients[index][:, :, None] * shifted_pixels(values_in, entry[0], entry[1])
        summed = term if summed is None else summed + term
    return shifted_pixels(values_in, 0, 0) - summed


def exchange_sum(block, axis, low_bit, bits):
    count = lax.axis_size(axis)
    received = [block]
    for offset in range(1, 1 << bits):
        flip = offset << low_bit
        route = [(i, i ^ flip) for i in range(count)]
        received.append(lax.ppermute(block, axis, route))
    while len(received) > 1:
        received = [received[i] + received[i + 1] for i in range(0, len(received), 2)]
    return received[0]


def all_sum(block, axis):
    count = lax.axis_size(axis)
    levels = count.bit_length() - 1
    if (1 << levels) != count:
        return lax.psum(block, axis)
    groups = []
    low_bit = 0
    while low_bit < levels:
        bits = min(2, levels - low_bit)
        groups.append((low_bit, bits))
        low_bit += bits
    for low_bit, bits in reversed(groups):
        block = exchange_sum(block, axis, low_bit, bits)
    return block


def per_device(intensity, agreement, basis_block):
    vectors, tile_rows, tile_cols = basis_block.shape
    row_count = lax.axis_size("row")
    col_count = lax.axis_size("col")
    total_rows = tile_rows * row_count
    total_cols = tile_cols * col_count
    labels = jnp.concatenate((intensity[None], agreement), axis=0)
    labels_wide = padded(labels, (("row", 1), ("col", 2)), 3)
    row_ids = lax.axis_index("row") * tile_rows + jnp.arange(-3, tile_rows + 3, dtype=jnp.int32)
    col_ids = lax.axis_index("col") * tile_cols + jnp.arange(-3, tile_cols + 3, dtype=jnp.int32)
    row_in = ((row_ids >= 0) & (row_ids < total_rows)).astype(jnp.float32)
    col_in = ((col_ids >= 0) & (col_ids < total_cols)).astype(jnp.float32)
    inside = row_in[:, None] * col_in[None, :]
    levels = labels_wide[0].astype(jnp.float32)
    counts = labels_wide[1:].astype(jnp.float32)
    weights = neighbour_weights(levels, counts, inside)
    scales = degree_scales(weights)
    row_ends = row_count - 1
    head = basis_block[:, :2, :]
    tail = basis_block[:, tile_rows - 2 :, :]
    from_above = lax.ppermute(tail, "row", [(i, i + 1) for i in range(row_ends)])
    from_below = lax.ppermute(head, "row", [(i + 1, i) for i in range(row_ends)])
    pixels = jnp.concatenate(
        [jnp.transpose(part, (1, 2, 0)) for part in (from_above, basis_block, from_below)], axis=0
    )
    extended = padded(pixels, (("col", 1),), 2)
    first = apply_pixels(extended, pass_coefficients([cropped(w, 1) for w in weights], scales))
    tile_scales = cropped(scales, 1)
    filtered = apply_pixels(first, pass_coefficients([cropped(w, 2) for w in weights], tile_scales))
    pixel_total = float(total_rows * total_cols)
    gram_local = jnp.einsum(
        "rck,rcj->kj", filtered, filtered,
        precision=lax.Precision.HIGHEST, preferred_element_type=jnp.float32,
    )
    gram = all_sum(all_sum(gram_local, "row"), "col") / pixel_total
    factor = jnp.linalg.cholesky(gram)
    inverse = jax.scipy.linalg.solve_triangular(
        factor, jnp.eye(vectors, dtype=jnp.float32), lower=True
    )
    ortho = jnp.einsum(
        "kj,rcj->krc", inverse, filtered,
        precision=lax.Precision.HIGHEST, preferred_element_type=jnp.float32,
    )
    return (ortho, factor.T)


def solution(mesh):
    return jax.shard_map(
        per_device,
        mesh=mesh,
        in_specs=(P("row", "col"), P(None, "row", "col"), P(None, "row", "col")),
        out_specs=(P(None, "row", "col"), P()),
        check_vma=False,
    )
```

```python
import jax
import jax.numpy as jnp
from jax import lax
from jax.sharding import PartitionSpec as P

INV_SIGMA = 1.0 / 40.0
NEIGHBOURS = (
    (0, 1, 0, 1, 1.0 / 9.0),
    (0, -1, 0, 0, 1.0 / 9.0),
    (1, 0, 1, 1, 1.0 / 9.0),
    (-1, 0, 1, 0, 1.0 / 9.0),
    (1, 1, 2, 1, 1.0 / 18.0),
    (-1, -1, 2, 0, 1.0 / 18.0),
    (1, -1, 3, 1, 1.0 / 18.0),
    (-1, 1, 3, 0, 1.0 / 18.0),
)


def padded(cells, sides, width):
    for axis, dim in sides:
        count = lax.axis_size(axis)
        ends = count - 1
        head = lax.slice_in_dim(cells, 0, width, axis=dim)
        tail = lax.slice_in_dim(cells, cells.shape[dim] - width, cells.shape[dim], axis=dim)
        cells = jnp.concatenate(
            [
                lax.ppermute(tail, axis, [(i, (i + 1) % count) for i in range(ends)]),
                cells,
                lax.ppermute(head, axis, [((i + 1) % count, i) for i in range(ends)]),
            ],
            axis=dim,
        )
    return cells


def shifted(array, step_row, step_col):
    height = array.shape[-2]
    width = array.shape[-1]
    return array[..., 1 + step_row : height - 1 + step_row, 1 + step_col : width - 1 + step_col]


def cropped(array, cycle):
    return array[..., cycle:-cycle, cycle:-cycle]


def neighbour_weights(levels, counts, inside):
    center = shifted(levels, 0, 0)
    center_in = shifted(inside, 0, 0)
    result = []
    for step_row, step_col, channel, at_center, factor in NEIGHBOURS:
        other = shifted(levels, step_row, step_col)
        if at_center == 1:
            source = shifted(counts[channel], 0, 0)
        else:
            source = shifted(counts[channel], step_row, step_col)
        gap = (center - other) * INV_SIGMA
        result.append(
            (1.0 + source)
            * factor
            * jnp.exp(-gap * gap)
            * center_in
            * shifted(inside, step_row, step_col)
        )
    return result


def degree_scales(weights):
    degree = weights[0]
    for weight in weights[1:]:
        degree = degree + weight
    return lax.rsqrt(1.0 + degree)


def apply_once(values_in, weights, scales):
    lifted = values_in * scales
    summed = None
    for weight, entry in zip(weights, NEIGHBOURS):
        term = weight * shifted(lifted, entry[0], entry[1])
        summed = term if summed is None else summed + term
    return shifted(values_in, 0, 0) - shifted(scales, 0, 0) * summed


def shifted_pixels(array, step_row, step_col):
    height = array.shape[0]
    width = array.shape[1]
    return array[1 + step_row : height - 1 + step_row, 1 + step_col : width - 1 + step_col]


def pass_coefficients(weights, scales):
    center = shifted(scales, 0, 0)
    return jnp.stack(
        [center * weight * shifted(scales, entry[0], entry[1]) for weight, entry in zip(weights, NEIGHBOURS)]
    )


def apply_pixels(values_in, coefficients):
    summed = None
    for index, entry in enumerate(NEIGHBOURS):
        term = coefficients[index][:, :, None] * shifted_pixels(values_in, entry[0], entry[1])
        summed = term if summed is None else summed + term
    return shifted_pixels(values_in, 0, 0) - summed


def exchange_sum(block, axis, low_bit, bits):
    count = lax.axis_size(axis)
    received = [block]
    for offset in range(1, 1 << bits):
        flip = offset << low_bit
        route = [(i, i ^ flip) for i in range(count)]
        received.append(lax.ppermute(block, axis, route))
    while len(received) > 1:
        received = [received[i] + received[i + 1] for i in range(0, len(received), 2)]
    return received[0]


def all_sum(block, axis, alone_low=False):
    count = lax.axis_size(axis)
    levels = count.bit_length() - 1
    if (1 << levels) != count:
        return lax.psum(block, axis)
    groups = []
    low_bit = 1 if alone_low and levels > 1 else 0
    if low_bit:
        groups.append((0, 1))
    while low_bit < levels:
        bits = min(2, levels - low_bit)
        groups.append((low_bit, bits))
        low_bit += bits
    for low_bit, bits in reversed(groups):
        block = exchange_sum(block, axis, low_bit, bits)
    return block


def per_device(intensity, agreement, basis_block):
    vectors, tile_rows, tile_cols = basis_block.shape
    row_count = lax.axis_size("row")
    col_count = lax.axis_size("col")
    total_rows = tile_rows * row_count
    total_cols = tile_cols * col_count
    labels = jnp.concatenate((intensity[None], agreement), axis=0)
    labels_wide = padded(labels, (("row", 1), ("col", 2)), 3)
    row_ids = lax.axis_index("row") * tile_rows + jnp.arange(-3, tile_rows + 3, dtype=jnp.int32)
    col_ids = lax.axis_index("col") * tile_cols + jnp.arange(-3, tile_cols + 3, dtype=jnp.int32)
    row_in = ((row_ids >= 0) & (row_ids < total_rows)).astype(jnp.float32)
    col_in = ((col_ids >= 0) & (col_ids < total_cols)).astype(jnp.float32)
    inside = row_in[:, None] * col_in[None, :]
    levels = labels_wide[0].astype(jnp.float32)
    counts = labels_wide[1:].astype(jnp.float32)
    weights = neighbour_weights(levels, counts, inside)
    scales = degree_scales(weights)
    pixels = jnp.transpose(basis_block, (1, 2, 0))
    extended = padded(pixels, (("row", 0), ("col", 1)), 2)
    first = apply_pixels(extended, pass_coefficients([cropped(w, 1) for w in weights], scales))
    tile_scales = cropped(scales, 1)
    filtered = apply_pixels(first, pass_coefficients([cropped(w, 2) for w in weights], tile_scales))
    pixel_total = float(total_rows * total_cols)
    gram_local = jnp.einsum(
        "rck,rcj->kj", filtered, filtered,
        precision=lax.Precision.HIGHEST, preferred_element_type=jnp.float32,
    )
    gram = all_sum(all_sum(gram_local, "row"), "col", alone_low=True) / pixel_total
    factor = jnp.linalg.cholesky(gram)
    inverse = jax.scipy.linalg.solve_triangular(
        factor, jnp.eye(vectors, dtype=jnp.float32), lower=True
    )
    ortho = jnp.einsum(
        "kj,rcj->krc", inverse, filtered,
        precision=lax.Precision.HIGHEST, preferred_element_type=jnp.float32,
    )
    return (ortho, factor.T)


def solution(mesh):
    return jax.shard_map(
        per_device,
        mesh=mesh,
        in_specs=(P("row", "col"), P(None, "row", "col"), P(None, "row", "col")),
        out_specs=(P(None, "row", "col"), P()),
        check_vma=False,
    )
```

```python
import jax
import jax.numpy as jnp
from jax import lax
from jax.sharding import PartitionSpec as P

INV_SIGMA = 1.0 / 40.0
NEIGHBOURS = (
    (0, 1, 0, 1, 1.0 / 9.0),
    (0, -1, 0, 0, 1.0 / 9.0),
    (1, 0, 1, 1, 1.0 / 9.0),
    (-1, 0, 1, 0, 1.0 / 9.0),
    (1, 1, 2, 1, 1.0 / 18.0),
    (-1, -1, 2, 0, 1.0 / 18.0),
    (1, -1, 3, 1, 1.0 / 18.0),
    (-1, 1, 3, 0, 1.0 / 18.0),
)


def padded(cells, sides, width):
    for axis, dim in sides:
        count = lax.axis_size(axis)
        ends = count - 1
        head = lax.slice_in_dim(cells, 0, width, axis=dim)
        tail = lax.slice_in_dim(cells, cells.shape[dim] - width, cells.shape[dim], axis=dim)
        cells = jnp.concatenate(
            [
                lax.ppermute(tail, axis, [(i, (i + 1) % count) for i in range(ends)]),
                cells,
                lax.ppermute(head, axis, [((i + 1) % count, i) for i in range(ends)]),
            ],
            axis=dim,
        )
    return cells


def shifted(array, step_row, step_col):
    height = array.shape[-2]
    width = array.shape[-1]
    return array[..., 1 + step_row : height - 1 + step_row, 1 + step_col : width - 1 + step_col]


def cropped(array, cycle):
    return array[..., cycle:-cycle, cycle:-cycle]


def neighbour_weights(levels, counts, inside):
    center = shifted(levels, 0, 0)
    center_in = shifted(inside, 0, 0)
    result = []
    for step_row, step_col, channel, at_center, factor in NEIGHBOURS:
        other = shifted(levels, step_row, step_col)
        if at_center == 1:
            source = shifted(counts[channel], 0, 0)
        else:
            source = shifted(counts[channel], step_row, step_col)
        gap = (center - other) * INV_SIGMA
        result.append(
            (1.0 + source)
            * factor
            * jnp.exp(-gap * gap)
            * center_in
            * shifted(inside, step_row, step_col)
        )
    return result


def degree_scales(weights):
    degree = weights[0]
    for weight in weights[1:]:
        degree = degree + weight
    return lax.rsqrt(1.0 + degree)


def apply_once(values_in, weights, scales):
    lifted = values_in * scales
    summed = None
    for weight, entry in zip(weights, NEIGHBOURS):
        term = weight * shifted(lifted, entry[0], entry[1])
        summed = term if summed is None else summed + term
    return shifted(values_in, 0, 0) - shifted(scales, 0, 0) * summed


def shifted_pixels(array, step_row, step_col):
    height = array.shape[0]
    width = array.shape[1]
    return array[1 + step_row : height - 1 + step_row, 1 + step_col : width - 1 + step_col]


def pass_coefficients(weights, scales):
    center = shifted(scales, 0, 0)
    return jnp.stack(
        [center * weight * shifted(scales, entry[0], entry[1]) for weight, entry in zip(weights, NEIGHBOURS)]
    )


def apply_pixels(values_in, coefficients):
    summed = None
    for index, entry in enumerate(NEIGHBOURS):
        term = coefficients[index][:, :, None] * shifted_pixels(values_in, entry[0], entry[1])
        summed = term if summed is None else summed + term
    return shifted_pixels(values_in, 0, 0) - summed


def exchange_sum(block, axis, low_bit, bits):
    count = lax.axis_size(axis)
    received = [block]
    for offset in range(1, 1 << bits):
        flip = offset << low_bit
        route = [(i, i ^ flip) for i in range(count)]
        received.append(lax.ppermute(block, axis, route))
    while len(received) > 1:
        received = [received[i] + received[i + 1] for i in range(0, len(received), 2)]
    return received[0]


def all_sum(block, axis):
    count = lax.axis_size(axis)
    levels = count.bit_length() - 1
    if (1 << levels) != count:
        return lax.psum(block, axis)
    groups = []
    low_bit = 0
    while low_bit < levels:
        bits = min(2, levels - low_bit)
        groups.append((low_bit, bits))
        low_bit += bits
    for low_bit, bits in reversed(groups):
        block = exchange_sum(block, axis, low_bit, bits)
    return block


def per_device(intensity, agreement, basis_block):
    vectors, tile_rows, tile_cols = basis_block.shape
    row_count = lax.axis_size("row")
    col_count = lax.axis_size("col")
    total_rows = tile_rows * row_count
    total_cols = tile_cols * col_count
    labels = jnp.concatenate((intensity[None], agreement), axis=0)
    labels_wide = padded(labels, (("row", 1), ("col", 2)), 3)
    row_ids = lax.axis_index("row") * tile_rows + jnp.arange(-3, tile_rows + 3, dtype=jnp.int32)
    col_ids = lax.axis_index("col") * tile_cols + jnp.arange(-3, tile_cols + 3, dtype=jnp.int32)
    row_in = ((row_ids >= 0) & (row_ids < total_rows)).astype(jnp.float32)
    col_in = ((col_ids >= 0) & (col_ids < total_cols)).astype(jnp.float32)
    inside = row_in[:, None] * col_in[None, :]
    levels = labels_wide[0].astype(jnp.float32)
    counts = labels_wide[1:].astype(jnp.float32)
    weights = neighbour_weights(levels, counts, inside)
    scales = degree_scales(weights)
    pixels = jnp.transpose(basis_block, (1, 2, 0))
    extended = padded(pixels, (("row", 0), ("col", 1)), 2)
    first = apply_pixels(extended, pass_coefficients([cropped(w, 1) for w in weights], scales))
    tile_scales = cropped(scales, 1)
    filtered = apply_pixels(first, pass_coefficients([cropped(w, 2) for w in weights], tile_scales))
    pixel_total = float(total_rows * total_cols)
    gram_local = jnp.einsum(
        "rck,rcj->kj", filtered, filtered,
        precision=lax.Precision.HIGHEST, preferred_element_type=jnp.float32,
    )
    gram = all_sum(all_sum(gram_local, "col"), "row") / pixel_total
    factor = jnp.linalg.cholesky(gram)
    inverse = jax.scipy.linalg.solve_triangular(
        factor, jnp.eye(vectors, dtype=jnp.float32), lower=True
    )
    ortho = jnp.einsum(
        "kj,rcj->krc", inverse, filtered,
        precision=lax.Precision.HIGHEST, preferred_element_type=jnp.float32,
    )
    return (ortho, factor.T)


def solution(mesh):
    return jax.shard_map(
        per_device,
        mesh=mesh,
        in_specs=(P("row", "col"), P(None, "row", "col"), P(None, "row", "col")),
        out_specs=(P(None, "row", "col"), P()),
        check_vma=False,
    )
```
